512 devices in a mesh: seq: 128 (over y, z, core), sub: 4 (over x).
Axes of the slice: x: 4, y: 8, z: 8, core: 2. Of those that a mesh axis runs over, the one named last changes fastest.
Arguments:
- linear_query: bfloat16 [32768, 256], P(('seq', 'sub')), may hold values from -6 to 6
- linear_key: bfloat16 [32768, 256], P(('seq', 'sub')), may hold values from -6 to 6
- linear_value: bfloat16 [32768, 2048], P(('seq', 'sub')), may hold values from -6 to 6
- lin_gain: float32 [2048], replicated, may hold values from 0.1 to 1.9
- window_query: bfloat16 [32768, 2048], P(('seq', 'sub')), may hold values from -6 to 6
- window_key: bfloat16 [32768, 2048], P(('seq', 'sub')), may hold values from -6 to 6
- window_value: bfloat16 [32768, 2048], P(('seq', 'sub')), may hold values from -6 to 6
Outputs:
- linear_out: bfloat16 [32768, 2048], P(('seq', 'sub'))
- window_out: bfloat16 [32768, 2048], P(('seq', 'sub'))
The draws below stay inside these ranges and needn't reach their ends.
All inputs are finite; a program needn't handle non-finite values.
Results may differ from the reference program's by a relative error of at most 0.007.
Values may be sent and summed in bfloat16 or wider, within the bound.
No kernel may reach another device: no remote copies, remote signals or barrier semaphores. Data moves between devices by JAX's collectives and lax.ppermute only.
A program may use at most 128 MiB of HBM per device.

```python
import math
import jax
import jax.numpy as jnp
from jax import lax

LHEADS = 16
SHEADS = 16
FDIM = 16
VDIM = 128
SDIM = 128
WINDOW = 512
FEAT = 273
TOKENS = 32768


def drawn_rows(key, for_query):
    full_shape = (TOKENS, SHEADS * SDIM)
    own_key = jax.random.fold_in(key, 11 if for_query else 13)
    drawn = jnp.clip(jax.random.normal(own_key, full_shape, jnp.float32), -6.0, 6.0)
    return drawn.astype(jnp.bfloat16)


def draw_window_query(key, part):
    return drawn_rows(key, True)


def draw_window_key(key, part):
    return drawn_rows(key, False)


def levels(rng, extent, cuts, low, top_value):
    def one(axis_at, parts):
        steps = jax.random.uniform(jax.random.fold_in(jax.random.fold_in(rng, 6), axis_at), (parts,), jnp.float32, low / len(cuts), top_value / len(cuts))
        return jnp.repeat(jnp.exp(steps), extent[axis_at] // parts).reshape((-1,) + (1,) * (len(extent) - axis_at - 1))

    loudness = one(*cuts[0])
    for cut in cuts[1:]:
        loudness = loudness * one(*cut)
    return loudness


def normal_values(stream_key, extent, spread, bound, cuts=(), held_as=jnp.bfloat16):
    values = jax.random.normal(stream_key, extent, jnp.float32) * spread
    if len(cuts) > 0:
        values = levels(stream_key, extent, cuts, -0.22, 0.18) * values
    return jnp.clip(values, min=-bound, max=bound).astype(held_as)


def setup_inputs(seed: int = 0) -> dict:
    streams_of = jax.random.split(jax.random.key(seed), 8)
    linear_query = normal_values(streams_of[0], (TOKENS, LHEADS * FDIM), 1.0, 6.0, ((0, 512),))
    linear_key = normal_values(streams_of[1], (TOKENS, LHEADS * FDIM), 1.0, 6.0, ((0, 512),))
    linear_value = normal_values(streams_of[2], (TOKENS, LHEADS * VDIM), 1.0, 6.0, ((0, 512),))
    lin_gain = jnp.clip(1.0 + 0.18 * jax.random.normal(streams_of[3], (LHEADS * VDIM,), jnp.float32), 0.1, 1.9)
    window_query = draw_window_query(jax.random.fold_in(streams_of[7], 71), 0)
    window_key = draw_window_key(jax.random.fold_in(streams_of[7], 71), 0)
    window_value = normal_values(streams_of[6], (TOKENS, SHEADS * SDIM), 1.0, 6.0, ((0, 512),))
    return {"linear_query": linear_query, "linear_key": linear_key, "linear_value": linear_value, "lin_gain": lin_gain, "window_query": window_query, "window_key": window_key, "window_value": window_value}


def features(vectors):
    halved = vectors * 0.5
    quadratic = halved[..., :, None] * halved[..., None, :]
    quadratic = quadratic.reshape(halved.shape[:-1] + (halved.shape[-1] * halved.shape[-1],)) * (1.0 / math.sqrt(2.0))
    constant = jnp.ones(halved.shape[:-1] + (1,), jnp.float32)
    return jnp.concatenate([constant, halved, quadratic], axis=-1)

def linear_part(linear_query, linear_key, linear_value, lin_gain):
    block_rows = min(512, TOKENS)
    block_count = TOKENS // block_rows
    query_all = linear_query.astype(jnp.float32).reshape(block_count, block_rows, LHEADS, FDIM)
    key_all = linear_key.astype(jnp.float32).reshape(block_count, block_rows, LHEADS, FDIM)
    value_all = linear_value.astype(jnp.float32).reshape(block_count, block_rows, LHEADS, VDIM)
    causal = jnp.arange(block_rows, dtype=jnp.int32)[:, None] >= jnp.arange(block_rows, dtype=jnp.int32)[None, :]

    def advance(carried, pieces):
        query_blk, key_blk, value_blk = pieces
        dot_inner = jnp.einsum('ihd,jhd->hij', query_blk, key_blk, precision=lax.Precision.HIGHEST) * 0.25
        weight = 1.0 + dot_inner + 0.5 * dot_inner * dot_inner
        weight = jnp.where(causal[None], weight, jnp.float32(0.0))
        local_sum = jnp.einsum('hij,jhe->ihe', weight, value_blk, precision=lax.Precision.HIGHEST)
        from_state = jnp.einsum('ihf,hfe->ihe', features(query_blk), carried, precision=lax.Precision.HIGHEST)
        carried = carried + jnp.einsum('jhf,jhe->hfe', features(key_blk), value_blk, precision=lax.Precision.HIGHEST)
        return (carried, local_sum + from_state)
    initial = jnp.zeros((LHEADS, FEAT, VDIM), jnp.float32)
    final_state, numerator = lax.scan(advance, initial, (query_all, key_all, value_all))
    numerator = numerator.reshape(TOKENS, LHEADS, VDIM)
    inv_rms = lax.rsqrt(lax.optimization_barrier(jnp.mean(numerator * numerator, axis=-1, keepdims=True)) + 1e-05)
    gain_rows = lin_gain.astype(jnp.float32).reshape(LHEADS, VDIM)
    return (numerator * inv_rms * gain_rows).reshape(TOKENS, LHEADS * VDIM).astype(jnp.bfloat16)

def window_part(window_query, window_key, window_value):
    block_rows = min(512, TOKENS)
    block_count = TOKENS // block_rows
    channels = SHEADS * SDIM
    padding = jnp.zeros((WINDOW, channels), jnp.bfloat16)
    key_padded = jnp.concatenate([padding, window_key], axis=0)
    value_padded = jnp.concatenate([padding, window_value], axis=0)

    def one_block(block_index):
        start = (block_index * block_rows).astype(jnp.int32)
        query_blk = lax.dynamic_slice_in_dim(window_query, start, block_rows, 0).reshape(block_rows, SHEADS, SDIM).astype(jnp.float32)
        key_blk = lax.dynamic_slice_in_dim(key_padded, start, WINDOW + block_rows, 0).reshape(WINDOW + block_rows, SHEADS, SDIM).astype(jnp.float32)
        value_blk = lax.dynamic_slice_in_dim(value_padded, start, WINDOW + block_rows, 0).reshape(WINDOW + block_rows, SHEADS, SDIM).astype(jnp.float32)
        scores = jnp.einsum('ihd,jhd->hij', query_blk, key_blk, precision=lax.Precision.HIGHEST) * (1.0 / math.sqrt(SDIM))
        query_pos = start + jnp.arange(block_rows, dtype=jnp.int32)
        key_pos = start - WINDOW + jnp.arange(WINDOW + block_rows, dtype=jnp.int32)
        allowed = (key_pos[None, :] <= query_pos[:, None]) & (key_pos[None, :] > query_pos[:, None] - WINDOW) & (key_pos[None, :] >= 0)
        scores = jnp.where(allowed[None], scores, jnp.float32(-1e+30))
        row_max = lax.optimization_barrier(jnp.max(scores, axis=-1, keepdims=True))
        exp_scores = jnp.exp(scores - row_max)
        weights_bf = (exp_scores / lax.optimization_barrier(jnp.sum(exp_scores, axis=-1, keepdims=True))).astype(jnp.bfloat16)
        mixed = jnp.einsum('hij,jhd->ihd', weights_bf.astype(jnp.float32), value_blk, precision=lax.Precision.HIGHEST)
        return mixed.reshape(block_rows, channels).astype(jnp.bfloat16)
    blocks_out = lax.map(one_block, jnp.arange(block_count, dtype=jnp.int32))
    return blocks_out.reshape(TOKENS, channels)

def reference(linear_query, linear_key, linear_value, lin_gain, window_query, window_key, window_value):
    linear_out = linear_part(linear_query, linear_key, linear_value, lin_gain)
    window_out = window_part(window_query, window_key, window_value)
    return (linear_out, window_out)
```

```python
import math

import jax
import jax.numpy as jnp
import numpy as np
from jax import lax
from jax.sharding import Mesh
from jax.sharding import PartitionSpec as P

FDIM = 16
VDIM = 128
SDIM = 128
WINDOW = 512
CORES = 2
ALL = ("outer", "core", "sub")
GROUP = ("core", "sub")


def passed_along(shard, axis, by):
    size = lax.axis_size(axis)
    pairs = [(i, i + by) for i in range(size) if 0 <= i + by < size]
    return lax.ppermute(shard, axis, pairs)


def sym_features(vectors, for_query):
    halved = vectors * 0.5
    pieces = [jnp.ones(halved.shape[:-1] + (1,), jnp.float32), halved]
    for a in range(FDIM):
        block = halved[..., a : a + 1] * halved[..., a:]
        if for_query:
            scale = np.ones((FDIM - a,), np.float32)
            scale[0] = 0.5
            block = block * scale
        pieces.append(block)
    return jnp.concatenate(pieces, axis=-1)


def shards(
    linear_query, linear_key, linear_value, lin_gain, window_query, window_key, window_value
):
    rows_dev = linear_query.shape[0]
    dev_count = lax.axis_size(ALL)
    group_count = lax.axis_size(GROUP)
    outer_count = lax.axis_size("outer")
    device_pos = lax.axis_index(ALL)
    base_row = device_pos * rows_dev
    reach_dev = WINDOW // rows_dev
    channels = window_key.shape[1]
    head_count = channels // SDIM
    lin_heads = linear_query.shape[1] // FDIM

    stacked = jnp.stack([window_key, window_value])
    earlier = [passed_along(stacked, ALL, reach_dev - t) for t in range(reach_dev)]
    earlier = jnp.concatenate(earlier, axis=1)
    key_rows = jnp.concatenate([earlier[0], window_key], axis=0).reshape(-1, head_count, SDIM)
    value_rows = jnp.concatenate([earlier[1], window_value], axis=0).reshape(-1, head_count, SDIM)

    query_bf = linear_query.reshape(rows_dev, lin_heads, FDIM)
    key_bf = linear_key.reshape(rows_dev, lin_heads, FDIM)
    query_lin = query_bf.astype(jnp.float32)
    key_lin = key_bf.astype(jnp.float32)
    value_lin = linear_value.astype(jnp.float32).reshape(rows_dev, lin_heads, VDIM)
    local_state = jnp.einsum(
        "jhf,jhe->hfe",
        sym_features(key_lin, False),
        value_lin,
        precision=lax.Precision.HIGHEST,
    )
    owned = lax.all_to_all(local_state[None], GROUP, split_axis=1, concat_axis=0, tiled=True)
    running_inner = jnp.cumsum(owned, axis=0)
    inner_before = running_inner - owned
    group_total = running_inner[-1]
    running = group_total
    for level in range((outer_count - 1).bit_length()):
        running = running + passed_along(running, "outer", 1 << level)
    groups_before = running - group_total
    slots = inner_before + groups_before[None]
    prefix = lax.all_to_all(slots, GROUP, split_axis=0, concat_axis=1, tiled=True)[0]

    query_heads = window_query.reshape(rows_dev, head_count, SDIM)
    scores = jnp.einsum(
        "ihd,jhd->hij", query_heads, key_rows, preferred_element_type=jnp.float32
    ) * (1.0 / math.sqrt(SDIM))
    query_pos = base_row + jnp.arange(rows_dev, dtype=jnp.int32)
    key_pos = (
        base_row - reach_dev * rows_dev + jnp.arange((reach_dev + 1) * rows_dev, dtype=jnp.int32)
    )
    allowed = (
        (key_pos[None, :] <= query_pos[:, None])
        & (key_pos[None, :] > query_pos[:, None] - WINDOW)
        & (key_pos[None, :] >= 0)
    )
    scores = jnp.where(allowed[None], scores, jnp.float32(-1e30))
    row_max = jnp.max(scores, axis=-1, keepdims=True)
    exp_scores = jnp.exp(scores - row_max)
    weights_bf = (exp_scores / jnp.sum(exp_scores, axis=-1, keepdims=True)).astype(jnp.bfloat16)
    mixed = jnp.einsum("hij,jhd->ihd", weights_bf, value_rows, preferred_element_type=jnp.float32)
    window_out = mixed.reshape(rows_dev, channels).astype(jnp.bfloat16)

    from_state = jnp.einsum(
        "ihf,hfe->ihe", sym_features(query_lin, True), prefix, precision=lax.Precision.HIGHEST
    )
    dot_inner = (
        jnp.einsum("ihd,jhd->hij", query_bf, key_bf, preferred_element_type=jnp.float32) * 0.25
    )
    weight = 1.0 + dot_inner + 0.5 * dot_inner * dot_inner
    causal = (
        jnp.arange(rows_dev, dtype=jnp.int32)[:, None]
        >= jnp.arange(rows_dev, dtype=jnp.int32)[None, :]
    )
    weight = jnp.where(causal[None], weight, jnp.float32(0.0))
    local_sum = jnp.einsum("hij,jhe->ihe", weight, value_lin, precision=lax.Precision.HIGHEST)
    numerator = local_sum + from_state
    inv_rms = lax.rsqrt(jnp.mean(numerator * numerator, axis=-1, keepdims=True) + 1e-05)
    gain_rows = lin_gain.reshape(lin_heads, VDIM)
    linear_out = (
        (numerator * inv_rms * gain_rows).reshape(rows_dev, lin_heads * VDIM).astype(jnp.bfloat16)
    )
    return (linear_out, window_out)


def solution(mesh):
    seq_count = mesh.shape["seq"]
    sub_count = mesh.shape["sub"]
    split_mesh = Mesh(
        np.asarray(mesh.devices).reshape(seq_count // CORES, CORES, sub_count), ALL
    )
    rows = P(ALL, None)
    in_specs = (rows, rows, rows, P(), rows, rows, rows)
    out_specs = (rows, rows)
    return jax.shard_map(
        shards, mesh=split_mesh, in_specs=in_specs, out_specs=out_specs, check_vma=False
    )
```

```python
import math

import jax
import jax.numpy as jnp
import numpy as np
from jax import lax
from jax.sharding import Mesh
from jax.sharding import PartitionSpec as P

FDIM = 16
VDIM = 128
SDIM = 128
WINDOW = 512
CORES = 2
ALL = ("y", "z", "core", "sub")
GROUP = ("core", "sub")


def pair_tables(for_query):
    pairs = [(0, 0)] + [(0, a + 1) for a in range(FDIM)]
    pairs += [(a + 1, b + 1) for a in range(FDIM) for b in range(a, FDIM)]
    first = np.zeros((FDIM + 1, len(pairs)), np.float32)
    second = np.zeros((FDIM + 1, len(pairs)), np.float32)
    for f, (a, b) in enumerate(pairs):
        first[a, f] = 0.5 if (for_query and a == b and a > 0) else 1.0
        second[b, f] = 1.0
    return first, second


def passed_along(shard, axis, by):
    size = lax.axis_size(axis)
    pairs = [(i, i + by) for i in range(size) if 0 <= i + by < size]
    return lax.ppermute(shard, axis, pairs)


def sym_features(vectors, for_query):
    halved = vectors * 0.5
    ext = jnp.concatenate([jnp.ones(halved.shape[:-1] + (1,), jnp.float32), halved], axis=-1)
    first, second = pair_tables(for_query)
    pick = lambda table: jnp.einsum(
        "jhi,if->jhf", ext, jnp.asarray(table), precision=lax.Precision.HIGHEST
    )
    return pick(first) * pick(second)


def shards(
    linear_query, linear_key, linear_value, lin_gain, window_query, window_key, window_value
):
    rows_dev = linear_query.shape[0]
    dev_count = lax.axis_size(ALL)
    group_count = lax.axis_size(GROUP)
    device_pos = lax.axis_index(ALL)
    base_row = device_pos * rows_dev
    reach_dev = WINDOW // rows_dev
    channels = window_key.shape[1]
    head_count = channels // SDIM
    lin_heads = linear_query.shape[1] // FDIM

    stacked = jnp.stack([window_key, window_value])
    earlier = [passed_along(stacked, ALL, reach_dev - t) for t in range(reach_dev)]
    earlier = jnp.concatenate(earlier, axis=1)
    key_rows = jnp.concatenate([earlier[0], window_key], axis=0).reshape(-1, head_count, SDIM)
    value_rows = jnp.concatenate([earlier[1], window_value], axis=0).reshape(-1, head_count, SDIM)

    query_bf = linear_query.reshape(rows_dev, lin_heads, FDIM)
    key_bf = linear_key.reshape(rows_dev, lin_heads, FDIM)
    query_lin = query_bf.astype(jnp.float32)
    key_lin = key_bf.astype(jnp.float32)
    value_lin = linear_value.astype(jnp.float32).reshape(rows_dev, lin_heads, VDIM)
    local_state = jnp.einsum(
        "jhf,jhe->hfe",
        sym_features(key_lin, False),
        value_lin,
        precision=lax.Precision.HIGHEST,
    )
    owned = lax.all_to_all(local_state[None], GROUP, split_axis=1, concat_axis=0, tiled=True)
    running_inner = jnp.cumsum(owned, axis=0)
    inner_before = running_inner - owned
    group_total = running_inner[-1]
    along_z = lax.all_gather(group_total, "z")
    z_before = jnp.arange(along_z.shape[0]) < lax.axis_index("z")
    line_before = jnp.sum(jnp.where(z_before[:, None, None, None], along_z, 0.0), axis=0)
    along_y = lax.all_gather(jnp.sum(along_z, axis=0), "y")
    y_before = jnp.arange(along_y.shape[0]) < lax.axis_index("y")
    groups_before = line_before + jnp.sum(
        jnp.where(y_before[:, None, None, None], along_y, 0.0), axis=0
    )
    slots = inner_before + groups_before[None]
    prefix = lax.all_to_all(slots, GROUP, split_axis=0, concat_axis=1, tiled=True)[0]

    query_heads = window_query.reshape(rows_dev, head_count, SDIM)
    scores = jnp.einsum(
        "ihd,jhd->hij", query_heads, key_rows, preferred_element_type=jnp.float32
    ) * (1.0 / math.sqrt(SDIM))
    query_pos = base_row + jnp.arange(rows_dev, dtype=jnp.int32)
    key_pos = (
        base_row - reach_dev * rows_dev + jnp.arange((reach_dev + 1) * rows_dev, dtype=jnp.int32)
    )
    allowed = (
        (key_pos[None, :] <= query_pos[:, None])
        & (key_pos[None, :] > query_pos[:, None] - WINDOW)
        & (key_pos[None, :] >= 0)
    )
    scores = jnp.where(allowed[None], scores, jnp.float32(-1e30))
    row_max = jnp.max(scores, axis=-1, keepdims=True)
    exp_scores = jnp.exp(scores - row_max)
    weights_bf = (exp_scores / jnp.sum(exp_scores, axis=-1, keepdims=True)).astype(jnp.bfloat16)
    mixed = jnp.einsum("hij,jhd->ihd", weights_bf, value_rows, preferred_element_type=jnp.float32)
    window_out = mixed.reshape(rows_dev, channels).astype(jnp.bfloat16)

    from_state = jnp.einsum(
        "ihf,hfe->ihe", sym_features(query_lin, True), prefix, precision=lax.Precision.HIGHEST
    )
    dot_inner = (
        jnp.einsum("ihd,jhd->hij", query_bf, key_bf, preferred_element_type=jnp.float32) * 0.25
    )
    weight = 1.0 + dot_inner + 0.5 * dot_inner * dot_inner
    causal = (
        jnp.arange(rows_dev, dtype=jnp.int32)[:, None]
        >= jnp.arange(rows_dev, dtype=jnp.int32)[None, :]
    )
    weight = jnp.where(causal[None], weight, jnp.float32(0.0))
    local_sum = jnp.einsum("hij,jhe->ihe", weight, value_lin, precision=lax.Precision.HIGHEST)
    numerator = local_sum + from_state
    inv_rms = lax.rsqrt(jnp.mean(numerator * numerator, axis=-1, keepdims=True) + 1e-05)
    gain_rows = lin_gain.reshape(lin_heads, VDIM)
    linear_out = (
        (numerator * inv_rms * gain_rows).reshape(rows_dev, lin_heads * VDIM).astype(jnp.bfloat16)
    )
    return (linear_out, window_out)


def solution(mesh):
    seq_count = mesh.shape["seq"]
    sub_count = mesh.shape["sub"]
    lines = seq_count // CORES
    z_count = math.isqrt(lines)
    split_mesh = Mesh(
        np.asarray(mesh.devices).reshape(lines // z_count, z_count, CORES, sub_count), ALL
    )
    rows = P(ALL, None)
    in_specs = (rows, rows, rows, P(), rows, rows, rows)
    out_specs = (rows, rows)
    return jax.shard_map(
        shards, mesh=split_mesh, in_specs=in_specs, out_specs=out_specs, check_vma=False
    )
```

```python
import math

import jax
import jax.numpy as jnp
import numpy as np
from jax import lax
from jax.sharding import Mesh
from jax.sharding import PartitionSpec as P

FDIM = 16
VDIM = 128
SDIM = 128
WINDOW = 512
CORES = 2
FEAT_PAD = 160
ALL = ("y", "z", "core", "sub")
GROUP = ("core", "sub")


def pair_tables(for_query):
    pairs = [(0, 0)] + [(0, a + 1) for a in range(FDIM)]
    pairs += [(a + 1, b + 1) for a in range(FDIM) for b in range(a, FDIM)]
    first = np.zeros((FDIM + 1, FEAT_PAD), np.float32)
    second = np.zeros((FDIM + 1, FEAT_PAD), np.float32)
    for f, (a, b) in enumerate(pairs):
        first[a, f] = 0.5 if (for_query and a == b and a > 0) else 1.0
        second[b, f] = 1.0
    return first, second


def passed_along(shard, axis, by):
    size = lax.axis_size(axis)
    pairs = [(i, i + by) for i in range(size) if 0 <= i + by < size]
    return lax.ppermute(shard, axis, pairs)


def sym_features(vectors, for_query):
    halved = vectors * 0.5
    ext = jnp.concatenate([jnp.ones(halved.shape[:-1] + (1,), jnp.float32), halved], axis=-1)
    first, second = pair_tables(for_query)
    pick = lambda table: jnp.einsum(
        "jhi,if->jhf", ext, jnp.asarray(table), precision=lax.Precision.HIGHEST
    )
    return pick(first) * pick(second)


def groups_before(total):
    z_count = lax.axis_size("z")
    heads, feats, width = total.shape
    dealt = total.reshape(heads, z_count, feats // z_count, width)
    held = lax.all_to_all(dealt, "z", split_axis=1, concat_axis=1, tiled=True)
    running = jnp.cumsum(held, axis=1)
    line_total = running[:, -1]
    along_y = lax.all_gather(line_total, "y")
    y_before = jnp.arange(along_y.shape[0]) < lax.axis_index("y")
    lines_before = jnp.sum(jnp.where(y_before[:, None, None, None], along_y, 0.0), axis=0)
    prefix = running - held + lines_before[:, None]
    back = lax.all_to_all(prefix, "z", split_axis=1, concat_axis=1, tiled=True)
    return back.reshape(heads, feats, width)


def linear_heads(linear_query, linear_key, linear_value, lin_gain):
    rows_dev = linear_query.shape[0]
    group_count = lax.axis_size(GROUP)
    lin_heads = linear_query.shape[1] // FDIM
    own_heads = lin_heads // group_count
    packed = jnp.concatenate(
        [
            linear_query.reshape(rows_dev, group_count, own_heads * FDIM),
            linear_key.reshape(rows_dev, group_count, own_heads * FDIM),
            linear_value.reshape(rows_dev, group_count, own_heads * VDIM),
        ],
        axis=-1,
    )
    got = lax.all_to_all(packed, GROUP, split_axis=1, concat_axis=0, tiled=True)
    rows = got.shape[0]
    got = got.reshape(rows, -1)
    query_bf = got[:, : own_heads * FDIM].reshape(rows, own_heads, FDIM)
    key_bf = got[:, own_heads * FDIM : 2 * own_heads * FDIM].reshape(rows, own_heads, FDIM)
    value_lin = got[:, 2 * own_heads * FDIM :].reshape(rows, own_heads, VDIM).astype(jnp.float32)
    query_lin = query_bf.astype(jnp.float32)
    key_lin = key_bf.astype(jnp.float32)
    total = jnp.einsum(
        "jhf,jhe->hfe", sym_features(key_lin, False), value_lin, precision=lax.Precision.HIGHEST
    )
    before = groups_before(total)
    from_state = jnp.einsum(
        "ihf,hfe->ihe", sym_features(query_lin, True), before, precision=lax.Precision.HIGHEST
    )
    dot_inner = (
        jnp.einsum("ihd,jhd->hij", query_bf, key_bf, preferred_element_type=jnp.float32) * 0.25
    )
    weight = 1.0 + dot_inner + 0.5 * dot_inner * dot_inner
    causal = jnp.arange(rows, dtype=jnp.int32)[:, None] >= jnp.arange(rows, dtype=jnp.int32)[None, :]
    weight = jnp.where(causal[None], weight, jnp.float32(0.0))
    local_sum = jnp.einsum("hij,jhe->ihe", weight, value_lin, precision=lax.Precision.HIGHEST)
    numerator = local_sum + from_state
    inv_rms = lax.rsqrt(jnp.mean(numerator * numerator, axis=-1, keepdims=True) + 1e-05)
    gain_rows = lax.dynamic_slice_in_dim(
        lin_gain.reshape(lin_heads, VDIM), lax.axis_index(GROUP) * own_heads, own_heads, 0
    )
    out = (numerator * inv_rms * gain_rows).astype(jnp.bfloat16)
    out = out.reshape(group_count, rows_dev, own_heads * VDIM)
    back = lax.all_to_all(out, GROUP, split_axis=0, concat_axis=2, tiled=True)
    return back.reshape(rows_dev, lin_heads * VDIM)


def shards(
    linear_query, linear_key, linear_value, lin_gain, window_query, window_key, window_value
):
    rows_dev = linear_query.shape[0]
    dev_count = lax.axis_size(ALL)
    group_count = lax.axis_size(GROUP)
    device_pos = lax.axis_index(ALL)
    base_row = device_pos * rows_dev
    reach_dev = WINDOW // rows_dev
    channels = window_key.shape[1]
    head_count = channels // SDIM
    lin_heads = linear_query.shape[1] // FDIM

    stacked = jnp.stack([window_key, window_value])
    earlier = [passed_along(stacked, ALL, reach_dev - t) for t in range(reach_dev)]
    earlier = jnp.concatenate(earlier, axis=1)
    key_rows = jnp.concatenate([earlier[0], window_key], axis=0).reshape(-1, head_count, SDIM)
    value_rows = jnp.concatenate([earlier[1], window_value], axis=0).reshape(-1, head_count, SDIM)

    query_heads = window_query.reshape(rows_dev, head_count, SDIM)
    scores = jnp.einsum(
        "ihd,jhd->hij", query_heads, key_rows, preferred_element_type=jnp.float32
    ) * (1.0 / math.sqrt(SDIM))
    query_pos = base_row + jnp.arange(rows_dev, dtype=jnp.int32)
    key_pos = (
        base_row - reach_dev * rows_dev + jnp.arange((reach_dev + 1) * rows_dev, dtype=jnp.int32)
    )
    allowed = (
        (key_pos[None, :] <= query_pos[:, None])
        & (key_pos[None, :] > query_pos[:, None] - WINDOW)
        & (key_pos[None, :] >= 0)
    )
    scores = jnp.where(allowed[None], scores, jnp.float32(-1e30))
    row_max = jnp.max(scores, axis=-1, keepdims=True)
    exp_scores = jnp.exp(scores - row_max)
    weights_bf = (exp_scores / jnp.sum(exp_scores, axis=-1, keepdims=True)).astype(jnp.bfloat16)
    mixed = jnp.einsum("hij,jhd->ihd", weights_bf, value_rows, preferred_element_type=jnp.float32)
    window_out = mixed.reshape(rows_dev, channels).astype(jnp.bfloat16)

    linear_out = linear_heads(linear_query, linear_key, linear_value, lin_gain)
    return (linear_out, window_out)


def solution(mesh):
    seq_count = mesh.shape["seq"]
    sub_count = mesh.shape["sub"]
    lines = seq_count // CORES
    z_count = math.isqrt(lines)
    split_mesh = Mesh(
        np.asarray(mesh.devices).reshape(lines // z_count, z_count, CORES, sub_count), ALL
    )
    rows = P(ALL, None)
    in_specs = (rows, rows, rows, P(), rows, rows, rows)
    out_specs = (rows, rows)
    return jax.shard_map(
        shards, mesh=split_mesh, in_specs=in_specs, out_specs=out_specs, check_vma=False
    )
```

```python
import functools
import math

import jax
import jax.numpy as jnp
import numpy as np
from jax import lax
from jax.experimental import pallas as pl
from jax.experimental.pallas import tpu as pltpu
from jax.sharding import Mesh
from jax.sharding import PartitionSpec as P

FDIM = 16
VDIM = 128
SDIM = 128
WINDOW = 512
CORES = 2
FEAT_PAD = 160
ALL = ("y", "z", "core", "sub")
GROUP = ("core", "sub")


def pair_tables(for_query):
    pairs = [(0, 0)] + [(0, a + 1) for a in range(FDIM)]
    pairs += [(a + 1, b + 1) for a in range(FDIM) for b in range(a, FDIM)]
    first = np.zeros((FDIM + 1, FEAT_PAD), np.float32)
    second = np.zeros((FDIM + 1, FEAT_PAD), np.float32)
    for f, (a, b) in enumerate(pairs):
        first[a, f] = 0.5 if (for_query and a == b and a > 0) else 1.0
        second[b, f] = 1.0
    return first, second


def passed_along(shard, axis, by):
    size = lax.axis_size(axis)
    pairs = [(i, i + by) for i in range(size) if 0 <= i + by < size]
    return lax.ppermute(shard, axis, pairs)


def sym_features(vectors, for_query):
    halved = vectors * 0.5
    ext = jnp.concatenate([jnp.ones(halved.shape[:-1] + (1,), jnp.float32), halved], axis=-1)
    first, second = pair_tables(for_query)
    pick = lambda table: jnp.einsum(
        "jhi,if->jhf", ext, jnp.asarray(table), precision=lax.Precision.HIGHEST
    )
    return pick(first) * pick(second)


def window_kernel(pos_ref, q_ref, k_ref, v_ref, *refs):
    reach = len(refs) - 1
    out_ref = refs[-1]
    rows = q_ref.shape[0]
    pos = pos_ref[0]
    row = lax.broadcasted_iota(jnp.int32, (rows, rows), 0)
    col = lax.broadcasted_iota(jnp.int32, (rows, rows), 1)
    here = jnp.zeros((rows, rows), jnp.int32) + pos
    scale = 1.0 / math.sqrt(SDIM)
    for head in range(q_ref.shape[1] // SDIM):
        lanes = pl.ds(head * SDIM, SDIM)
        query = q_ref[:, lanes]
        keys = [refs[t][0, :, lanes] for t in range(reach)] + [k_ref[:, lanes]]
        values = [refs[t][1, :, lanes] for t in range(reach)] + [v_ref[:, lanes]]
        scores = []
        for t in range(reach + 1):
            s = lax.dot_general(query, keys[t], (((1,), (1,)), ((), ())),
                                preferred_element_type=jnp.float32) * scale
            if t == reach:
                ok = col <= row
            elif t == 0:
                ok = (col > row) & (here >= reach - t)
            else:
                ok = here >= reach - t
            scores.append(jnp.where(ok, s, jnp.float32(-1e30)))
        top = functools.reduce(jnp.maximum, [jnp.max(s, axis=1, keepdims=True) for s in scores])
        expd = [jnp.exp(s - top) for s in scores]
        total = functools.reduce(jnp.add, [jnp.sum(e, axis=1, keepdims=True) for e in expd])
        acc = None
        for t in range(reach + 1):
            part = lax.dot_general((expd[t] / total).astype(jnp.bfloat16), values[t],
                                   (((1,), (0,)), ((), ())), preferred_element_type=jnp.float32)
            acc = part if acc is None else acc + part
        out_ref[:, lanes] = acc.astype(out_ref.dtype)

def window_attention(pos, query, key, value, earlier):
    rows, channels = query.shape
    lanes = 4 * SDIM
    steps = channels // lanes
    flat = pl.BlockSpec((rows, lanes), lambda g, p: (0, g))
    stacked = pl.BlockSpec((2, rows, lanes), lambda g, p: (0, 0, g))
    return pl.pallas_call(
        window_kernel,
        out_shape=jax.ShapeDtypeStruct((rows, channels), jnp.bfloat16),
        grid_spec=pltpu.PrefetchScalarGridSpec(
            num_scalar_prefetch=1, grid=(steps,),
            in_specs=[flat, flat, flat] + [stacked] * len(earlier),
            out_specs=flat),
    )(jnp.reshape(pos, (1,)).astype(jnp.int32), query, key, value, *earlier)


def groups_before(total):
    z_count = lax.axis_size("z")
    heads, feats, width = total.shape
    dealt = total.reshape(heads, z_count, feats // z_count, width)
    held = lax.all_to_all(dealt, "z", split_axis=1, concat_axis=1, tiled=True)
    running = jnp.cumsum(held, axis=1)
    line_total = running[:, -1]
    along_y = lax.all_gather(line_total, "y")
    y_before = jnp.arange(along_y.shape[0]) < lax.axis_index("y")
    lines_before = jnp.sum(jnp.where(y_before[:, None, None, None], along_y, 0.0), axis=0)
    prefix = running - held + lines_before[:, None]
    back = lax.all_to_all(prefix, "z", split_axis=1, concat_axis=1, tiled=True)
    return back.reshape(heads, feats, width)


def linear_heads(linear_query, linear_key, linear_value, lin_gain):
    rows_dev = linear_query.shape[0]
    group_count = lax.axis_size(GROUP)
    lin_heads = linear_query.shape[1] // FDIM
    own_heads = lin_heads // group_count
    packed = jnp.concatenate(
        [
            linear_query.reshape(rows_dev, group_count, own_heads * FDIM),
            linear_key.reshape(rows_dev, group_count, own_heads * FDIM),
            linear_value.reshape(rows_dev, group_count, own_heads * VDIM),
        ],
        axis=-1,
    )
    got = lax.all_to_all(packed, GROUP, split_axis=1, concat_axis=0, tiled=True)
    rows = got.shape[0]
    got = got.reshape(rows, -1)
    query_bf = got[:, : own_heads * FDIM].reshape(rows, own_heads, FDIM)
    key_bf = got[:, own_heads * FDIM : 2 * own_heads * FDIM].reshape(rows, own_heads, FDIM)
    value_lin = got[:, 2 * own_heads * FDIM :].reshape(rows, own_heads, VDIM).astype(jnp.float32)
    query_lin = query_bf.astype(jnp.float32)
    key_lin = key_bf.astype(jnp.float32)
    total = jnp.einsum(
        "jhf,jhe->hfe", sym_features(key_lin, False), value_lin, precision=lax.Precision.HIGHEST
    )
    before = groups_before(total)
    from_state = jnp.einsum(
        "ihf,hfe->ihe", sym_features(query_lin, True), before, precision=lax.Precision.HIGHEST
    )
    dot_inner = (
        jnp.einsum("ihd,jhd->hij", query_bf, key_bf, preferred_element_type=jnp.float32) * 0.25
    )
    weight = 1.0 + dot_inner + 0.5 * dot_inner * dot_inner
    causal = jnp.arange(rows, dtype=jnp.int32)[:, None] >= jnp.arange(rows, dtype=jnp.int32)[None, :]
    weight = jnp.where(causal[None], weight, jnp.float32(0.0))
    local_sum = jnp.einsum("hij,jhe->ihe", weight, value_lin, precision=lax.Precision.HIGHEST)
    numerator = local_sum + from_state
    inv_rms = lax.rsqrt(jnp.mean(numerator * numerator, axis=-1, keepdims=True) + 1e-05)
    gain_rows = lax.dynamic_slice_in_dim(
        lin_gain.reshape(lin_heads, VDIM), lax.axis_index(GROUP) * own_heads, own_heads, 0
    )
    out = (numerator * inv_rms * gain_rows).astype(jnp.bfloat16)
    out = out.reshape(group_count, rows_dev, own_heads * VDIM)
    back = lax.all_to_all(out, GROUP, split_axis=0, concat_axis=2, tiled=True)
    return back.reshape(rows_dev, lin_heads * VDIM)


def shards(
    linear_query, linear_key, linear_value, lin_gain, window_query, window_key, window_value
):
    rows_dev = linear_query.shape[0]
    dev_count = lax.axis_size(ALL)
    group_count = lax.axis_size(GROUP)
    device_pos = lax.axis_index(ALL)
    base_row = device_pos * rows_dev
    reach_dev = WINDOW // rows_dev
    channels = window_key.shape[1]
    head_count = channels // SDIM
    lin_heads = linear_query.shape[1] // FDIM

    stacked = jnp.stack([window_key, window_value])
    earlier = [passed_along(stacked, ALL, reach_dev - t) for t in range(reach_dev)]
    window_out = window_attention(device_pos, window_query, window_key, window_value, earlier)
    linear_out = linear_heads(linear_query, linear_key, linear_value, lin_gain)
    return (linear_out, window_out)


def solution(mesh):
    seq_count = mesh.shape["seq"]
    sub_count = mesh.shape["sub"]
    lines = seq_count // CORES
    z_count = math.isqrt(lines)
    split_mesh = Mesh(
        np.asarray(mesh.devices).reshape(lines // z_count, z_count, CORES, sub_count), ALL
    )
    rows = P(ALL, None)
    in_specs = (rows, rows, rows, P(), rows, rows, rows)
    out_specs = (rows, rows)
    return jax.shard_map(
        shards, mesh=split_mesh, in_specs=in_specs, out_specs=out_specs, check_vma=False
    )
```

```python
import functools
import math

import jax
import jax.numpy as jnp
import numpy as np
from jax import lax
from jax.experimental import pallas as pl
from jax.experimental.pallas import tpu as pltpu
from jax.sharding import Mesh
from jax.sharding import PartitionSpec as P

FDIM = 16
VDIM = 128
SDIM = 128
WINDOW = 512
CORES = 2
FEAT_PAD = 160
ALL = ("y", "z", "core", "sub")
GROUP = ("core", "sub")


def pair_tables(for_query):
    pairs = [(0, 0)] + [(0, a + 1) for a in range(FDIM)]
    pairs += [(a + 1, b + 1) for a in range(FDIM) for b in range(a, FDIM)]
    first = np.zeros((FDIM + 1, FEAT_PAD), np.float32)
    second = np.zeros((FDIM + 1, FEAT_PAD), np.float32)
    for f, (a, b) in enumerate(pairs):
        first[a, f] = 0.5 if (for_query and a == b and a > 0) else 1.0
        second[b, f] = 1.0
    return first, second


def passed_along(shard, axis, by):
    size = lax.axis_size(axis)
    pairs = [(i, i + by) for i in range(size) if 0 <= i + by < size]
    return lax.ppermute(shard, axis, pairs)


def sym_features(vectors, for_query):
    halved = vectors * 0.5
    ext = jnp.concatenate([jnp.ones(halved.shape[:-1] + (1,), jnp.float32), halved], axis=-1)
    first, second = pair_tables(for_query)
    pick = lambda table: jnp.einsum(
        "jhi,if->jhf", ext, jnp.asarray(table), precision=lax.Precision.HIGHEST
    )
    return pick(first) * pick(second)


def window_kernel(pos_ref, q_ref, k_ref, v_ref, *refs):
    reach = len(refs) - 1
    out_ref = refs[-1]
    rows = q_ref.shape[0]
    pos = pos_ref[0]
    row = lax.broadcasted_iota(jnp.int32, (rows, rows), 0)
    col = lax.broadcasted_iota(jnp.int32, (rows, rows), 1)
    here = jnp.zeros((rows, rows), jnp.int32) + pos
    scale = 1.0 / math.sqrt(SDIM)
    for head in range(q_ref.shape[1] // SDIM):
        lanes = pl.ds(head * SDIM, SDIM)
        query = q_ref[:, lanes]
        keys = [refs[t][0, :, lanes] for t in range(reach)] + [k_ref[:, lanes]]
        values = [refs[t][1, :, lanes] for t in range(reach)] + [v_ref[:, lanes]]
        scores = []
        for t in range(reach + 1):
            s = lax.dot_general(query, keys[t], (((1,), (1,)), ((), ())),
                                preferred_element_type=jnp.float32) * scale
            if t == reach:
                ok = col <= row
            elif t == 0:
                ok = (col > row) & (here >= reach - t)
            else:
                ok = here >= reach - t
            scores.append(jnp.where(ok, s, jnp.float32(-1e30)))
        top = functools.reduce(jnp.maximum, [jnp.max(s, axis=1, keepdims=True) for s in scores])
        expd = [jnp.exp(s - top) for s in scores]
        total = functools.reduce(jnp.add, [jnp.sum(e, axis=1, keepdims=True) for e in expd])
        acc = None
        for t in range(reach + 1):
            part = lax.dot_general((expd[t] / total).astype(jnp.bfloat16), values[t],
                                   (((1,), (0,)), ((), ())), preferred_element_type=jnp.float32)
            acc = part if acc is None else acc + part
        out_ref[:, lanes] = acc.astype(out_ref.dtype)

def window_attention(pos, query, key, value, earlier):
    rows, channels = query.shape
    lanes = 4 * SDIM
    steps = channels // lanes
    flat = pl.BlockSpec((rows, lanes), lambda g, p: (0, g))
    stacked = pl.BlockSpec((2, rows, lanes), lambda g, p: (0, 0, g))
    return pl.pallas_call(
        window_kernel,
        out_shape=jax.ShapeDtypeStruct((rows, channels), jnp.bfloat16),
        grid_spec=pltpu.PrefetchScalarGridSpec(
            num_scalar_prefetch=1, grid=(steps,),
            in_specs=[flat, flat, flat] + [stacked] * len(earlier),
            out_specs=flat),
    )(jnp.reshape(pos, (1,)).astype(jnp.int32), query, key, value, *earlier)


def groups_before(total):
    z_count = lax.axis_size("z")
    heads, feats, width = total.shape
    dealt = total.reshape(heads, z_count, feats // z_count, width)
    held = lax.all_to_all(dealt, "z", split_axis=1, concat_axis=1, tiled=True)
    running = jnp.cumsum(held, axis=1)
    line_total = running[:, -1]
    along_y = lax.all_gather(line_total, "y")
    y_before = jnp.arange(along_y.shape[0]) < lax.axis_index("y")
    lines_before = jnp.sum(jnp.where(y_before[:, None, None, None], along_y, 0.0), axis=0)
    prefix = running - held + lines_before[:, None]
    back = lax.all_to_all(prefix, "z", split_axis=1, concat_axis=1, tiled=True)
    return back.reshape(heads, feats, width)


def linear_heads(linear_query, linear_key, linear_value, lin_gain, held):
    rows_dev = linear_query.shape[0]
    group_count = lax.axis_size(GROUP)
    lin_heads = linear_query.shape[1] // FDIM
    own_heads = lin_heads // group_count
    packed = jnp.concatenate(
        [
            linear_query.reshape(rows_dev, group_count, own_heads * FDIM),
            linear_key.reshape(rows_dev, group_count, own_heads * FDIM),
            linear_value.reshape(rows_dev, group_count, own_heads * VDIM),
        ],
        axis=-1,
    )
    got = lax.all_to_all(packed, GROUP, split_axis=1, concat_axis=0, tiled=True)
    rows = got.shape[0]
    got = got.reshape(rows, -1)
    query_bf = got[:, : own_heads * FDIM].reshape(rows, own_heads, FDIM)
    key_bf = got[:, own_heads * FDIM : 2 * own_heads * FDIM].reshape(rows, own_heads, FDIM)
    value_lin = got[:, 2 * own_heads * FDIM :].reshape(rows, own_heads, VDIM).astype(jnp.float32)
    query_lin = query_bf.astype(jnp.float32)
    key_lin = key_bf.astype(jnp.float32)
    total = jnp.einsum(
        "jhf,jhe->hfe", sym_features(key_lin, False), value_lin, precision=lax.Precision.HIGHEST
    )
    before, held = lax.optimization_barrier((groups_before(total), held))
    from_state = jnp.einsum(
        "ihf,hfe->ihe", sym_features(query_lin, True), before, precision=lax.Precision.HIGHEST
    )
    dot_inner = (
        jnp.einsum("ihd,jhd->hij", query_bf, key_bf, preferred_element_type=jnp.float32) * 0.25
    )
    weight = 1.0 + dot_inner + 0.5 * dot_inner * dot_inner
    causal = jnp.arange(rows, dtype=jnp.int32)[:, None] >= jnp.arange(rows, dtype=jnp.int32)[None, :]
    weight = jnp.where(causal[None], weight, jnp.float32(0.0))
    local_sum = jnp.einsum("hij,jhe->ihe", weight, value_lin, precision=lax.Precision.HIGHEST)
    numerator = local_sum + from_state
    inv_rms = lax.rsqrt(jnp.mean(numerator * numerator, axis=-1, keepdims=True) + 1e-05)
    gain_rows = lax.dynamic_slice_in_dim(
        lin_gain.reshape(lin_heads, VDIM), lax.axis_index(GROUP) * own_heads, own_heads, 0
    )
    out = (numerator * inv_rms * gain_rows).astype(jnp.bfloat16)
    out = out.reshape(group_count, rows_dev, own_heads * VDIM)
    back = lax.all_to_all(out, GROUP, split_axis=0, concat_axis=2, tiled=True)
    return back.reshape(rows_dev, lin_heads * VDIM), held


def shards(
    linear_query, linear_key, linear_value, lin_gain, window_query, window_key, window_value
):
    rows_dev = linear_query.shape[0]
    dev_count = lax.axis_size(ALL)
    group_count = lax.axis_size(GROUP)
    device_pos = lax.axis_index(ALL)
    base_row = device_pos * rows_dev
    reach_dev = WINDOW // rows_dev
    channels = window_key.shape[1]
    head_count = channels // SDIM
    lin_heads = linear_query.shape[1] // FDIM

    stacked = jnp.stack([window_key, window_value])
    linear_out, stacked = linear_heads(linear_query, linear_key, linear_value, lin_gain, stacked)
    earlier = [passed_along(stacked, ALL, reach_dev - t) for t in range(reach_dev)]
    window_out = window_attention(device_pos, window_query, window_key, window_value, earlier)
    return (linear_out, window_out)


def solution(mesh):
    seq_count = mesh.shape["seq"]
    sub_count = mesh.shape["sub"]
    lines = seq_count // CORES
    z_count = math.isqrt(lines)
    split_mesh = Mesh(
        np.asarray(mesh.devices).reshape(lines // z_count, z_count, CORES, sub_count), ALL
    )
    rows = P(ALL, None)
    in_specs = (rows, rows, rows, P(), rows, rows, rows)
    out_specs = (rows, rows)
    return jax.shard_map(
        shards, mesh=split_mesh, in_specs=in_specs, out_specs=out_specs, check_vma=False
    )
```

```python
import functools
import math

import jax
import jax.numpy as jnp
import numpy as np
from jax import lax
from jax.experimental import pallas as pl
from jax.experimental.pallas import tpu as pltpu
from jax.sharding import Mesh
from jax.sharding import PartitionSpec as P

FDIM = 16
VDIM = 128
SDIM = 128
WINDOW = 512
CORES = 2
FEAT_PAD = 160
ALL = ("y", "z", "core", "sub")
GROUP = ("core", "sub")


def pair_tables(for_query):
    pairs = [(0, 0)] + [(0, a + 1) for a in range(FDIM)]
    pairs += [(a + 1, b + 1) for a in range(FDIM) for b in range(a, FDIM)]
    first = np.zeros((FDIM + 1, FEAT_PAD), np.float32)
    second = np.zeros((FDIM + 1, FEAT_PAD), np.float32)
    for f, (a, b) in enumerate(pairs):
        first[a, f] = 0.5 if (for_query and a == b and a > 0) else 1.0
        second[b, f] = 1.0
    return first, second


def passed_along(shard, axis, by):
    size = lax.axis_size(axis)
    pairs = [(i, i + by) for i in range(size) if 0 <= i + by < size]
    return lax.ppermute(shard, axis, pairs)


def sym_features(vectors, for_query):
    halved = vectors * 0.5
    ext = jnp.concatenate([jnp.ones(halved.shape[:-1] + (1,), jnp.float32), halved], axis=-1)
    first, second = pair_tables(for_query)
    pick = lambda table: jnp.einsum(
        "jhi,if->jhf", ext, jnp.asarray(table), precision=lax.Precision.HIGHEST
    )
    return pick(first) * pick(second)


def window_kernel(pos_ref, q_ref, k_ref, v_ref, *refs):
    reach = len(refs) - 1
    out_ref = refs[-1]
    rows = q_ref.shape[0]
    pos = pos_ref[0]
    row = lax.broadcasted_iota(jnp.int32, (rows, rows), 0)
    col = lax.broadcasted_iota(jnp.int32, (rows, rows), 1)
    here = jnp.zeros((rows, rows), jnp.int32) + pos
    scale = 1.0 / math.sqrt(SDIM)
    for head in range(q_ref.shape[1] // SDIM):
        lanes = pl.ds(head * SDIM, SDIM)
        query = q_ref[:, lanes]
        keys = [refs[t][0, :, lanes] for t in range(reach)] + [k_ref[:, lanes]]
        values = [refs[t][1, :, lanes] for t in range(reach)] + [v_ref[:, lanes]]
        scores = []
        for t in range(reach + 1):
            s = lax.dot_general(query, keys[t], (((1,), (1,)), ((), ())),
                                preferred_element_type=jnp.float32) * scale
            if t == reach:
                ok = col <= row
            elif t == 0:
                ok = (col > row) & (here >= reach - t)
            else:
                ok = here >= reach - t
            scores.append(jnp.where(ok, s, jnp.float32(-1e30)))
        top = functools.reduce(jnp.maximum, [jnp.max(s, axis=1, keepdims=True) for s in scores])
        expd = [jnp.exp(s - top) for s in scores]
        total = functools.reduce(jnp.add, [jnp.sum(e, axis=1, keepdims=True) for e in expd])
        acc = None
        for t in range(reach + 1):
            part = lax.dot_general((expd[t] / total).astype(jnp.bfloat16), values[t],
                                   (((1,), (0,)), ((), ())), preferred_element_type=jnp.float32)
            acc = part if acc is None else acc + part
        out_ref[:, lanes] = acc.astype(out_ref.dtype)

def window_attention(pos, query, key, value, earlier):
    rows, channels = query.shape
    lanes = 4 * SDIM
    steps = channels // lanes
    flat = pl.BlockSpec((rows, lanes), lambda g, p: (0, g))
    stacked = pl.BlockSpec((2, rows, lanes), lambda g, p: (0, 0, g))
    return pl.pallas_call(
        window_kernel,
        out_shape=jax.ShapeDtypeStruct((rows, channels), jnp.bfloat16),
        grid_spec=pltpu.PrefetchScalarGridSpec(
            num_scalar_prefetch=1, grid=(steps,),
            in_specs=[flat, flat, flat] + [stacked] * len(earlier),
            out_specs=flat),
    )(jnp.reshape(pos, (1,)).astype(jnp.int32), query, key, value, *earlier)


def groups_before(total):
    z_count = lax.axis_size("z")
    heads, feats, width = total.shape
    dealt = total.reshape(heads, z_count, feats // z_count, width)
    held = lax.all_to_all(dealt, "z", split_axis=1, concat_axis=1, tiled=True)
    running = jnp.cumsum(held, axis=1)
    line_total = running[:, -1]
    lines = line_total
    for level in range((lax.axis_size("y") - 1).bit_length()):
        lines = lines + passed_along(lines, "y", 1 << level)
    lines_before = lines - line_total
    prefix = running - held + lines_before[:, None]
    back = lax.all_to_all(prefix, "z", split_axis=1, concat_axis=1, tiled=True)
    return back.reshape(heads, feats, width)


def linear_heads(linear_query, linear_key, linear_value, lin_gain, held):
    rows_dev = linear_query.shape[0]
    group_count = lax.axis_size(GROUP)
    lin_heads = linear_query.shape[1] // FDIM
    own_heads = lin_heads // group_count
    packed = jnp.concatenate(
        [
            linear_query.reshape(rows_dev, group_count, own_heads * FDIM),
            linear_key.reshape(rows_dev, group_count, own_heads * FDIM),
            linear_value.reshape(rows_dev, group_count, own_heads * VDIM),
        ],
        axis=-1,
    )
    got = lax.all_to_all(packed, GROUP, split_axis=1, concat_axis=0, tiled=True)
    rows = got.shape[0]
    got = got.reshape(rows, -1)
    query_bf = got[:, : own_heads * FDIM].reshape(rows, own_heads, FDIM)
    key_bf = got[:, own_heads * FDIM : 2 * own_heads * FDIM].reshape(rows, own_heads, FDIM)
    value_lin = got[:, 2 * own_heads * FDIM :].reshape(rows, own_heads, VDIM).astype(jnp.float32)
    query_lin = query_bf.astype(jnp.float32)
    key_lin = key_bf.astype(jnp.float32)
    total = jnp.einsum(
        "jhf,jhe->hfe", sym_features(key_lin, False), value_lin, precision=lax.Precision.HIGHEST
    )
    before, held = lax.optimization_barrier((groups_before(total), held))
    from_state = jnp.einsum(
        "ihf,hfe->ihe", sym_features(query_lin, True), before, precision=lax.Precision.HIGHEST
    )
    dot_inner = (
        jnp.einsum("ihd,jhd->hij", query_bf, key_bf, preferred_element_type=jnp.float32) * 0.25
    )
    weight = 1.0 + dot_inner + 0.5 * dot_inner * dot_inner
    causal = jnp.arange(rows, dtype=jnp.int32)[:, None] >= jnp.arange(rows, dtype=jnp.int32)[None, :]
    weight = jnp.where(causal[None], weight, jnp.float32(0.0))
    local_sum = jnp.einsum("hij,jhe->ihe", weight, value_lin, precision=lax.Precision.HIGHEST)
    numerator = local_sum + from_state
    inv_rms = lax.rsqrt(jnp.mean(numerator * numerator, axis=-1, keepdims=True) + 1e-05)
    gain_rows = lax.dynamic_slice_in_dim(
        lin_gain.reshape(lin_heads, VDIM), lax.axis_index(GROUP) * own_heads, own_heads, 0
    )
    out = (numerator * inv_rms * gain_rows).astype(jnp.bfloat16)
    out = out.reshape(group_count, rows_dev, own_heads * VDIM)
    back = lax.all_to_all(out, GROUP, split_axis=0, concat_axis=2, tiled=True)
    return back.reshape(rows_dev, lin_heads * VDIM), held


def shards(
    linear_query, linear_key, linear_value, lin_gain, window_query, window_key, window_value
):
    rows_dev = linear_query.shape[0]
    dev_count = lax.axis_size(ALL)
    group_count = lax.axis_size(GROUP)
    device_pos = lax.axis_index(ALL)
    base_row = device_pos * rows_dev
    reach_dev = WINDOW // rows_dev
    channels = window_key.shape[1]
    head_count = channels // SDIM
    lin_heads = linear_query.shape[1] // FDIM

    stacked = jnp.stack([window_key, window_value])
    linear_out, stacked = linear_heads(linear_query, linear_key, linear_value, lin_gain, stacked)
    earlier = [passed_along(stacked, ALL, reach_dev - t) for t in range(reach_dev)]
    window_out = window_attention(device_pos, window_query, window_key, window_value, earlier)
    return (linear_out, window_out)


def solution(mesh):
    seq_count = mesh.shape["seq"]
    sub_count = mesh.shape["sub"]
    lines = seq_count // CORES
    z_count = math.isqrt(lines)
    split_mesh = Mesh(
        np.asarray(mesh.devices).reshape(lines // z_count, z_count, CORES, sub_count), ALL
    )
    rows = P(ALL, None)
    in_specs = (rows, rows, rows, P(), rows, rows, rows)
    out_specs = (rows, rows)
    return jax.shard_map(
        shards, mesh=split_mesh, in_specs=in_specs, out_specs=out_specs, check_vma=False
    )
```

```python
import functools
import math

import jax
import jax.numpy as jnp
import numpy as np
from jax import lax
from jax.experimental import pallas as pl
from jax.experimental.pallas import tpu as pltpu
from jax.sharding import Mesh
from jax.sharding import PartitionSpec as P

FDIM = 16
VDIM = 128
SDIM = 128
WINDOW = 512
CORES = 2
FEAT_PAD = 160
ALL = ("y", "z", "core", "sub")
GROUP = ("core", "sub")


def pair_tables(for_query):
    pairs = [(0, 0)] + [(0, a + 1) for a in range(FDIM)]
    pairs += [(a + 1, b + 1) for a in range(FDIM) for b in range(a, FDIM)]
    first = np.zeros((FDIM + 1, FEAT_PAD), np.float32)
    second = np.zeros((FDIM + 1, FEAT_PAD), np.float32)
    for f, (a, b) in enumerate(pairs):
        first[a, f] = 0.5 if (for_query and a == b and a > 0) else 1.0
        second[b, f] = 1.0
    return first, second


def passed_along(shard, axis, by):
    size = lax.axis_size(axis)
    pairs = [(i, i + by) for i in range(size) if 0 <= i + by < size]
    return lax.ppermute(shard, axis, pairs)


def sym_features(vectors, for_query):
    halved = vectors * 0.5
    ext = jnp.concatenate([jnp.ones(halved.shape[:-1] + (1,), jnp.float32), halved], axis=-1)
    first, second = pair_tables(for_query)
    pick = lambda table: jnp.einsum(
        "jhi,if->jhf", ext, jnp.asarray(table), precision=lax.Precision.HIGHEST
    )
    return pick(first) * pick(second)


def window_kernel(pos_ref, q_ref, k_ref, v_ref, *refs):
    reach = len(refs) - 1
    out_ref = refs[-1]
    rows = q_ref.shape[0]
    pos = pos_ref[0]
    row = lax.broadcasted_iota(jnp.int32, (rows, rows), 0)
    col = lax.broadcasted_iota(jnp.int32, (rows, rows), 1)
    here = jnp.zeros((rows, rows), jnp.int32) + pos
    scale = 1.0 / math.sqrt(SDIM)
    for head in range(q_ref.shape[1] // SDIM):
        lanes = pl.ds(head * SDIM, SDIM)
        query = q_ref[:, lanes]
        keys = [refs[t][0, :, lanes] for t in range(reach)] + [k_ref[:, lanes]]
        values = [refs[t][1, :, lanes] for t in range(reach)] + [v_ref[:, lanes]]
        scores = []
        for t in range(reach + 1):
            s = lax.dot_general(query, keys[t], (((1,), (1,)), ((), ())),
                                preferred_element_type=jnp.float32) * scale
            if t == reach:
                ok = col <= row
            elif t == 0:
                ok = (col > row) & (here >= reach - t)
            else:
                ok = here >= reach - t
            scores.append(jnp.where(ok, s, jnp.float32(-1e30)))
        top = functools.reduce(jnp.maximum, [jnp.max(s, axis=1, keepdims=True) for s in scores])
        expd = [jnp.exp(s - top) for s in scores]
        total = functools.reduce(jnp.add, [jnp.sum(e, axis=1, keepdims=True) for e in expd])
        acc = None
        for t in range(reach + 1):
            part = lax.dot_general((expd[t] / total).astype(jnp.bfloat16), values[t],
                                   (((1,), (0,)), ((), ())), preferred_element_type=jnp.float32)
            acc = part if acc is None else acc + part
        out_ref[:, lanes] = acc.astype(out_ref.dtype)

def window_attention(pos, query, key, value, earlier):
    rows, channels = query.shape
    lanes = 4 * SDIM
    steps = channels // lanes
    flat = pl.BlockSpec((rows, lanes), lambda g, p: (0, g))
    stacked = pl.BlockSpec((2, rows, lanes), lambda g, p: (0, 0, g))
    return pl.pallas_call(
        window_kernel,
        out_shape=jax.ShapeDtypeStruct((rows, channels), jnp.bfloat16),
        grid_spec=pltpu.PrefetchScalarGridSpec(
            num_scalar_prefetch=1, grid=(steps,),
            in_specs=[flat, flat, flat] + [stacked] * len(earlier),
            out_specs=flat),
    )(jnp.reshape(pos, (1,)).astype(jnp.int32), query, key, value, *earlier)


def groups_before(total):
    outer = ("y", "z")
    outer_count = lax.axis_size(outer)
    shape = total.shape
    dealt = total.reshape(outer_count, -1, shape[-1])
    held = lax.all_to_all(dealt, outer, split_axis=0, concat_axis=0, tiled=True)
    prefix = jnp.cumsum(held, axis=0) - held
    back = lax.all_to_all(prefix, outer, split_axis=0, concat_axis=0, tiled=True)
    return back.reshape(shape)


def linear_heads(linear_query, linear_key, linear_value, lin_gain, held):
    rows_dev = linear_query.shape[0]
    group_count = lax.axis_size(GROUP)
    lin_heads = linear_query.shape[1] // FDIM
    own_heads = lin_heads // group_count
    packed = jnp.concatenate(
        [
            linear_query.reshape(rows_dev, group_count, own_heads * FDIM),
            linear_key.reshape(rows_dev, group_count, own_heads * FDIM),
            linear_value.reshape(rows_dev, group_count, own_heads * VDIM),
        ],
        axis=-1,
    )
    got = lax.all_to_all(packed, GROUP, split_axis=1, concat_axis=0, tiled=True)
    rows = got.shape[0]
    got = got.reshape(rows, -1)
    query_bf = got[:, : own_heads * FDIM].reshape(rows, own_heads, FDIM)
    key_bf = got[:, own_heads * FDIM : 2 * own_heads * FDIM].reshape(rows, own_heads, FDIM)
    value_lin = got[:, 2 * own_heads * FDIM :].reshape(rows, own_heads, VDIM).astype(jnp.float32)
    query_lin = query_bf.astype(jnp.float32)
    key_lin = key_bf.astype(jnp.float32)
    total = jnp.einsum(
        "jhf,jhe->hfe", sym_features(key_lin, False), value_lin, precision=lax.Precision.HIGHEST
    )
    before, held = lax.optimization_barrier((groups_before(total), held))
    from_state = jnp.einsum(
        "ihf,hfe->ihe", sym_features(query_lin, True), before, precision=lax.Precision.HIGHEST
    )
    dot_inner = (
        jnp.einsum("ihd,jhd->hij", query_bf, key_bf, preferred_element_type=jnp.float32) * 0.25
    )
    weight = 1.0 + dot_inner + 0.5 * dot_inner * dot_inner
    causal = jnp.arange(rows, dtype=jnp.int32)[:, None] >= jnp.arange(rows, dtype=jnp.int32)[None, :]
    weight = jnp.where(causal[None], weight, jnp.float32(0.0))
    local_sum = jnp.einsum("hij,jhe->ihe", weight, value_lin, precision=lax.Precision.HIGHEST)
    numerator = local_sum + from_state
    inv_rms = lax.rsqrt(jnp.mean(numerator * numerator, axis=-1, keepdims=True) + 1e-05)
    gain_rows = lax.dynamic_slice_in_dim(
        lin_gain.reshape(lin_heads, VDIM), lax.axis_index(GROUP) * own_heads, own_heads, 0
    )
    out = (numerator * inv_rms * gain_rows).astype(jnp.bfloat16)
    out = out.reshape(group_count, rows_dev, own_heads * VDIM)
    back = lax.all_to_all(out, GROUP, split_axis=0, concat_axis=2, tiled=True)
    return back.reshape(rows_dev, lin_heads * VDIM), held


def shards(
    linear_query, linear_key, linear_value, lin_gain, window_query, window_key, window_value
):
    rows_dev = linear_query.shape[0]
    dev_count = lax.axis_size(ALL)
    group_count = lax.axis_size(GROUP)
    device_pos = lax.axis_index(ALL)
    base_row = device_pos * rows_dev
    reach_dev = WINDOW // rows_dev
    channels = window_key.shape[1]
    head_count = channels // SDIM
    lin_heads = linear_query.shape[1] // FDIM

    stacked = jnp.stack([window_key, window_value])
    linear_out, stacked = linear_heads(linear_query, linear_key, linear_value, lin_gain, stacked)
    earlier = [passed_along(stacked, ALL, reach_dev - t) for t in range(reach_dev)]
    window_out = window_attention(device_pos, window_query, window_key, window_value, earlier)
    return (linear_out, window_out)


def solution(mesh):
    seq_count = mesh.shape["seq"]
    sub_count = mesh.shape["sub"]
    lines = seq_count // CORES
    z_count = math.isqrt(lines)
    split_mesh = Mesh(
        np.asarray(mesh.devices).reshape(lines // z_count, z_count, CORES, sub_count), ALL
    )
    rows = P(ALL, None)
    in_specs = (rows, rows, rows, P(), rows, rows, rows)
    out_specs = (rows, rows)
    return jax.shard_map(
        shards, mesh=split_mesh, in_specs=in_specs, out_specs=out_specs, check_vma=False
    )
```

```python
import functools
import math

import jax
import jax.numpy as jnp
import numpy as np
from jax import lax
from jax.experimental import pallas as pl
from jax.experimental.pallas import tpu as pltpu
from jax.sharding import Mesh
from jax.sharding import PartitionSpec as P

FDIM = 16
VDIM = 128
SDIM = 128
WINDOW = 512
CORES = 2
FEAT_PAD = 160
ALL = ("y", "z", "core", "sub")
GROUP = ("core", "sub")


def pair_tables(for_query):
    pairs = [(0, 0)] + [(0, a + 1) for a in range(FDIM)]
    pairs += [(a + 1, b + 1) for a in range(FDIM) for b in range(a, FDIM)]
    first = np.zeros((FDIM + 1, FEAT_PAD), np.float32)
    second = np.zeros((FDIM + 1, FEAT_PAD), np.float32)
    for f, (a, b) in enumerate(pairs):
        first[a, f] = 0.5 if (for_query and a == b and a > 0) else 1.0
        second[b, f] = 1.0
    return first, second


def passed_along(shard, axis, by):
    size = lax.axis_size(axis)
    pairs = [(i, i + by) for i in range(size) if 0 <= i + by < size]
    return lax.ppermute(shard, axis, pairs)


def sym_features(vectors, for_query):
    halved = vectors * 0.5
    ext = jnp.concatenate([jnp.ones(halved.shape[:-1] + (1,), jnp.float32), halved], axis=-1)
    first, second = pair_tables(for_query)
    pick = lambda table: jnp.einsum(
        "jhi,if->jhf", ext, jnp.asarray(table), precision=lax.Precision.HIGHEST
    )
    return pick(first) * pick(second)


def window_kernel(pos_ref, q_ref, k_ref, v_ref, *refs):
    reach = len(refs) - 1
    out_ref = refs[-1]
    rows = q_ref.shape[0]
    pos = pos_ref[0]
    row = lax.broadcasted_iota(jnp.int32, (rows, rows), 0)
    col = lax.broadcasted_iota(jnp.int32, (rows, rows), 1)
    here = jnp.zeros((rows, rows), jnp.int32) + pos
    scale = 1.0 / math.sqrt(SDIM)
    for head in range(q_ref.shape[1] // SDIM):
        lanes = pl.ds(head * SDIM, SDIM)
        query = q_ref[:, lanes]
        keys = [refs[t][0, :, lanes] for t in range(reach)] + [k_ref[:, lanes]]
        values = [refs[t][1, :, lanes] for t in range(reach)] + [v_ref[:, lanes]]
        scores = []
        for t in range(reach + 1):
            s = lax.dot_general(query, keys[t], (((1,), (1,)), ((), ())),
                                preferred_element_type=jnp.float32) * scale
            if t == reach:
                ok = col <= row
            elif t == 0:
                ok = (col > row) & (here >= reach - t)
            else:
                ok = here >= reach - t
            scores.append(jnp.where(ok, s, jnp.float32(-1e30)))
        top = functools.reduce(jnp.maximum, [jnp.max(s, axis=1, keepdims=True) for s in scores])
        expd = [jnp.exp(s - top) for s in scores]
        total = functools.reduce(jnp.add, [jnp.sum(e, axis=1, keepdims=True) for e in expd])
        acc = None
        for t in range(reach + 1):
            part = lax.dot_general((expd[t] / total).astype(jnp.bfloat16), values[t],
                                   (((1,), (0,)), ((), ())), preferred_element_type=jnp.float32)
            acc = part if acc is None else acc + part
        out_ref[:, lanes] = acc.astype(out_ref.dtype)

def window_attention(pos, query, key, value, earlier):
    rows, channels = query.shape
    lanes = 4 * SDIM
    steps = channels // lanes
    flat = pl.BlockSpec((rows, lanes), lambda g, p: (0, g))
    stacked = pl.BlockSpec((2, rows, lanes), lambda g, p: (0, 0, g))
    return pl.pallas_call(
        window_kernel,
        out_shape=jax.ShapeDtypeStruct((rows, channels), jnp.bfloat16),
        grid_spec=pltpu.PrefetchScalarGridSpec(
            num_scalar_prefetch=1, grid=(steps,),
            in_specs=[flat, flat, flat] + [stacked] * len(earlier),
            out_specs=flat),
    )(jnp.reshape(pos, (1,)).astype(jnp.int32), query, key, value, *earlier)


def groups_before(total):
    outer = ("y", "z")
    outer_count = lax.axis_size(outer)
    shape = total.shape
    dealt = total.reshape(outer_count, -1, shape[-1])
    held = lax.all_to_all(dealt, outer, split_axis=0, concat_axis=0, tiled=True)
    prefix = jnp.cumsum(held, axis=0) - held
    back = lax.all_to_all(prefix, outer, split_axis=0, concat_axis=0, tiled=True)
    return back.reshape(shape)


def linear_heads(linear_query, linear_key, linear_value, lin_gain, held):
    rows_dev = linear_query.shape[0]
    group_count = lax.axis_size(GROUP)
    lin_heads = linear_query.shape[1] // FDIM
    own_heads = lin_heads // group_count
    packed = jnp.concatenate(
        [
            linear_query.reshape(rows_dev, group_count, own_heads * FDIM),
            linear_key.reshape(rows_dev, group_count, own_heads * FDIM),
            linear_value.reshape(rows_dev, group_count, own_heads * VDIM),
        ],
        axis=-1,
    )
    got = lax.all_to_all(packed, GROUP, split_axis=1, concat_axis=0, tiled=True)
    got, held = lax.optimization_barrier((got, held))
    rows = got.shape[0]
    got = got.reshape(rows, -1)
    query_bf = got[:, : own_heads * FDIM].reshape(rows, own_heads, FDIM)
    key_bf = got[:, own_heads * FDIM : 2 * own_heads * FDIM].reshape(rows, own_heads, FDIM)
    value_lin = got[:, 2 * own_heads * FDIM :].reshape(rows, own_heads, VDIM).astype(jnp.float32)
    query_lin = query_bf.astype(jnp.float32)
    key_lin = key_bf.astype(jnp.float32)
    total = jnp.einsum(
        "jhf,jhe->hfe", sym_features(key_lin, False), value_lin, precision=lax.Precision.HIGHEST
    )
    before = groups_before(total)
    from_state = jnp.einsum(
        "ihf,hfe->ihe", sym_features(query_lin, True), before, precision=lax.Precision.HIGHEST
    )
    dot_inner = (
        jnp.einsum("ihd,jhd->hij", query_bf, key_bf, preferred_element_type=jnp.float32) * 0.25
    )
    weight = 1.0 + dot_inner + 0.5 * dot_inner * dot_inner
    causal = jnp.arange(rows, dtype=jnp.int32)[:, None] >= jnp.arange(rows, dtype=jnp.int32)[None, :]
    weight = jnp.where(causal[None], weight, jnp.float32(0.0))
    local_sum = jnp.einsum("hij,jhe->ihe", weight, value_lin, precision=lax.Precision.HIGHEST)
    numerator = local_sum + from_state
    inv_rms = lax.rsqrt(jnp.mean(numerator * numerator, axis=-1, keepdims=True) + 1e-05)
    gain_rows = lax.dynamic_slice_in_dim(
        lin_gain.reshape(lin_heads, VDIM), lax.axis_index(GROUP) * own_heads, own_heads, 0
    )
    out = (numerator * inv_rms * gain_rows).astype(jnp.bfloat16)
    out = out.reshape(group_count, rows_dev, own_heads * VDIM)
    back = lax.all_to_all(out, GROUP, split_axis=0, concat_axis=2, tiled=True)
    return back.reshape(rows_dev, lin_heads * VDIM), held


def shards(
    linear_query, linear_key, linear_value, lin_gain, window_query, window_key, window_value
):
    rows_dev = linear_query.shape[0]
    dev_count = lax.axis_size(ALL)
    group_count = lax.axis_size(GROUP)
    device_pos = lax.axis_index(ALL)
    base_row = device_pos * rows_dev
    reach_dev = WINDOW // rows_dev
    channels = window_key.shape[1]
    head_count = channels // SDIM
    lin_heads = linear_query.shape[1] // FDIM

    stacked = jnp.stack([window_key, window_value])
    linear_out, stacked = linear_heads(linear_query, linear_key, linear_value, lin_gain, stacked)
    earlier = [passed_along(stacked, ALL, reach_dev - t) for t in range(reach_dev)]
    window_out = window_attention(device_pos, window_query, window_key, window_value, earlier)
    return (linear_out, window_out)


def solution(mesh):
    seq_count = mesh.shape["seq"]
    sub_count = mesh.shape["sub"]
    lines = seq_count // CORES
    z_count = math.isqrt(lines)
    split_mesh = Mesh(
        np.asarray(mesh.devices).reshape(lines // z_count, z_count, CORES, sub_count), ALL
    )
    rows = P(ALL, None)
    in_specs = (rows, rows, rows, P(), rows, rows, rows)
    out_specs = (rows, rows)
    return jax.shard_map(
        shards, mesh=split_mesh, in_specs=in_specs, out_specs=out_specs, check_vma=False
    )
```

```python
import math

import jax
import jax.numpy as jnp
import numpy as np
from jax import lax
from jax.experimental import pallas as pl
from jax.experimental.pallas import tpu as pltpu
from jax.sharding import Mesh
from jax.sharding import PartitionSpec as P

FDIM = 16
VDIM = 128
SDIM = 128
WINDOW = 512
CORES = 2
FEAT_PAD = 160
ALL = ("y", "z", "core", "sub")
GROUP = ("core", "sub")


def pair_tables(for_query):
    pairs = [(0, 0)] + [(0, a + 1) for a in range(FDIM)]
    pairs += [(a + 1, b + 1) for a in range(FDIM) for b in range(a, FDIM)]
    first = np.zeros((FDIM + 1, FEAT_PAD), np.float32)
    second = np.zeros((FDIM + 1, FEAT_PAD), np.float32)
    for f, (a, b) in enumerate(pairs):
        first[a, f] = 0.5 if (for_query and a == b and a > 0) else 1.0
        second[b, f] = 1.0
    return first, second


def passed_along(shard, axis, by):
    size = lax.axis_size(axis)
    pairs = [(i, i + by) for i in range(size) if 0 <= i + by < size]
    return lax.ppermute(shard, axis, pairs)


def sym_features(vectors, for_query):
    halved = vectors * 0.5
    ext = jnp.concatenate([jnp.ones(halved.shape[:-1] + (1,), jnp.float32), halved], axis=-1)
    first, second = pair_tables(for_query)
    pick = lambda table: jnp.einsum(
        "jhi,if->jhf", ext, jnp.asarray(table), precision=lax.Precision.HIGHEST
    )
    return pick(first) * pick(second)


def window_kernel(pos_ref, q_ref, k_ref, v_ref, *refs):
    reach = len(refs) - 1
    out_ref = refs[-1]
    rows = q_ref.shape[0]
    span = (reach + 1) * rows
    row = lax.broadcasted_iota(jnp.int32, (rows, span), 0)
    rel = lax.broadcasted_iota(jnp.int32, (rows, span), 1) - reach * rows
    first = jnp.zeros((rows, span), jnp.int32) + pos_ref[0] * rows
    allowed = (rel <= row) & (rel > row - WINDOW) & (first + rel >= 0)
    scale = 1.0 / math.sqrt(SDIM)
    for head in range(q_ref.shape[1] // SDIM):
        lanes = pl.ds(head * SDIM, SDIM)
        keys = jnp.concatenate([refs[t][0, :, lanes] for t in range(reach)] + [k_ref[:, lanes]], axis=0)
        values = jnp.concatenate([refs[t][1, :, lanes] for t in range(reach)] + [v_ref[:, lanes]], axis=0)
        scores = lax.dot_general(q_ref[:, lanes], keys, (((1,), (1,)), ((), ())),
                                 preferred_element_type=jnp.float32) * scale
        scores = jnp.where(allowed, scores, jnp.float32(-1e30))
        expd = jnp.exp(scores - jnp.max(scores, axis=1, keepdims=True))
        probs = (expd / jnp.sum(expd, axis=1, keepdims=True)).astype(jnp.bfloat16)
        out_ref[:, lanes] = lax.dot_general(probs, values, (((1,), (0,)), ((), ())),
                                            preferred_element_type=jnp.float32).astype(out_ref.dtype)

def window_attention(pos, query, key, value, earlier):
    rows, channels = query.shape
    lanes = 4 * SDIM
    steps = channels // lanes
    flat = pl.BlockSpec((rows, lanes), lambda g, p: (0, g))
    stacked = pl.BlockSpec((2, rows, lanes), lambda g, p: (0, 0, g))
    return pl.pallas_call(
        window_kernel,
        out_shape=jax.ShapeDtypeStruct((rows, channels), jnp.bfloat16),
        grid_spec=pltpu.PrefetchScalarGridSpec(
            num_scalar_prefetch=1, grid=(steps,),
            in_specs=[flat, flat, flat] + [stacked] * len(earlier),
            out_specs=flat),
    )(jnp.reshape(pos, (1,)).astype(jnp.int32), query, key, value, *earlier)


def groups_before(total):
    outer = ("y", "z")
    outer_count = lax.axis_size(outer)
    shape = total.shape
    dealt = total.reshape(outer_count, -1, shape[-1])
    held = lax.all_to_all(dealt, outer, split_axis=0, concat_axis=0, tiled=True)
    prefix = jnp.cumsum(held, axis=0) - held
    back = lax.all_to_all(prefix, outer, split_axis=0, concat_axis=0, tiled=True)
    return back.reshape(shape)


def linear_heads(linear_query, linear_key, linear_value, lin_gain, held):
    rows_dev = linear_query.shape[0]
    group_count = lax.axis_size(GROUP)
    lin_heads = linear_query.shape[1] // FDIM
    own_heads = lin_heads // group_count
    packed = jnp.concatenate(
        [
            linear_query.reshape(rows_dev, group_count, own_heads * FDIM),
            linear_key.reshape(rows_dev, group_count, own_heads * FDIM),
            linear_value.reshape(rows_dev, group_count, own_heads * VDIM),
        ],
        axis=-1,
    )
    got = lax.all_to_all(packed, GROUP, split_axis=1, concat_axis=0, tiled=True)
    got, held = lax.optimization_barrier((got, held))
    rows = got.shape[0]
    got = got.reshape(rows, -1)
    query_bf = got[:, : own_heads * FDIM].reshape(rows, own_heads, FDIM)
    key_bf = got[:, own_heads * FDIM : 2 * own_heads * FDIM].reshape(rows, own_heads, FDIM)
    value_lin = got[:, 2 * own_heads * FDIM :].reshape(rows, own_heads, VDIM).astype(jnp.float32)
    query_lin = query_bf.astype(jnp.float32)
    key_lin = key_bf.astype(jnp.float32)
    total = jnp.einsum(
        "jhf,jhe->hfe", sym_features(key_lin, False), value_lin, precision=lax.Precision.HIGHEST
    )
    before = groups_before(total)
    from_state = jnp.einsum(
        "ihf,hfe->ihe", sym_features(query_lin, True), before, precision=lax.Precision.HIGHEST
    )
    dot_inner = (
        jnp.einsum("ihd,jhd->hij", query_bf, key_bf, preferred_element_type=jnp.float32) * 0.25
    )
    weight = 1.0 + dot_inner + 0.5 * dot_inner * dot_inner
    causal = jnp.arange(rows, dtype=jnp.int32)[:, None] >= jnp.arange(rows, dtype=jnp.int32)[None, :]
    weight = jnp.where(causal[None], weight, jnp.float32(0.0))
    local_sum = jnp.einsum("hij,jhe->ihe", weight, value_lin, precision=lax.Precision.HIGHEST)
    numerator = local_sum + from_state
    inv_rms = lax.rsqrt(jnp.mean(numerator * numerator, axis=-1, keepdims=True) + 1e-05)
    gain_rows = lax.dynamic_slice_in_dim(
        lin_gain.reshape(lin_heads, VDIM), lax.axis_index(GROUP) * own_heads, own_heads, 0
    )
    out = (numerator * inv_rms * gain_rows).astype(jnp.bfloat16)
    out = out.reshape(group_count, rows_dev, own_heads * VDIM)
    back = lax.all_to_all(out, GROUP, split_axis=0, concat_axis=2, tiled=True)
    return back.reshape(rows_dev, lin_heads * VDIM), held


def shards(
    linear_query, linear_key, linear_value, lin_gain, window_query, window_key, window_value
):
    rows_dev = linear_query.shape[0]
    dev_count = lax.axis_size(ALL)
    group_count = lax.axis_size(GROUP)
    device_pos = lax.axis_index(ALL)
    base_row = device_pos * rows_dev
    reach_dev = WINDOW // rows_dev
    channels = window_key.shape[1]
    head_count = channels // SDIM
    lin_heads = linear_query.shape[1] // FDIM

    stacked = jnp.stack([window_key, window_value])
    linear_out, stacked = linear_heads(linear_query, linear_key, linear_value, lin_gain, stacked)
    earlier = [passed_along(stacked, ALL, reach_dev - t) for t in range(reach_dev)]
    window_out = window_attention(device_pos, window_query, window_key, window_value, earlier)
    return (linear_out, window_out)


def solution(mesh):
    seq_count = mesh.shape["seq"]
    sub_count = mesh.shape["sub"]
    lines = seq_count // CORES
    z_count = math.isqrt(lines)
    split_mesh = Mesh(
        np.asarray(mesh.devices).reshape(lines // z_count, z_count, CORES, sub_count), ALL
    )
    rows = P(ALL, None)
    in_specs = (rows, rows, rows, P(), rows, rows, rows)
    out_specs = (rows, rows)
    return jax.shard_map(
        shards, mesh=split_mesh, in_specs=in_specs, out_specs=out_specs, check_vma=False
    )
```

```python
import math

import jax
import jax.numpy as jnp
import numpy as np
from jax import lax
from jax.experimental import pallas as pl
from jax.experimental.pallas import tpu as pltpu
from jax.sharding import Mesh
from jax.sharding import PartitionSpec as P

FDIM = 16
VDIM = 128
SDIM = 128
WINDOW = 512
CORES = 2
FEAT_PAD = 160
ALL = ("y", "z", "core", "sub")
GROUP = ("core", "sub")


def pair_tables(for_query):
    pairs = [(0, 0)] + [(0, a + 1) for a in range(FDIM)]
    pairs += [(a + 1, b + 1) for a in range(FDIM) for b in range(a, FDIM)]
    first = np.zeros((FDIM + 1, FEAT_PAD), np.float32)
    second = np.zeros((FDIM + 1, FEAT_PAD), np.float32)
    for f, (a, b) in enumerate(pairs):
        first[a, f] = 0.5 if (for_query and a == b and a > 0) else 1.0
        second[b, f] = 1.0
    return first, second


def passed_along(shard, axis, by):
    size = lax.axis_size(axis)
    pairs = [(i, i + by) for i in range(size) if 0 <= i + by < size]
    return lax.ppermute(shard, axis, pairs)


def sym_features(vectors, for_query):
    halved = vectors * 0.5
    ext = jnp.concatenate([jnp.ones(halved.shape[:-1] + (1,), jnp.float32), halved], axis=-1)
    first, second = pair_tables(for_query)
    pick = lambda table: jnp.einsum(
        "jhi,if->jhf", ext, jnp.asarray(table), precision=lax.Precision.HIGHEST
    )
    return pick(first) * pick(second)


def window_kernel(pos_ref, q_ref, k_ref, v_ref, *refs):
    reach = len(refs) - 1
    out_ref = refs[-1]
    rows = q_ref.shape[0]
    span = (reach + 1) * rows
    row = lax.broadcasted_iota(jnp.int32, (rows, span), 0)
    rel = lax.broadcasted_iota(jnp.int32, (rows, span), 1) - reach * rows
    first = jnp.zeros((rows, span), jnp.int32) + pos_ref[0] * rows
    allowed = (rel <= row) & (rel > row - WINDOW) & (first + rel >= 0)
    scale = 1.0 / math.sqrt(SDIM)
    for head in range(q_ref.shape[1] // SDIM):
        lanes = pl.ds(head * SDIM, SDIM)
        keys = jnp.concatenate([refs[t][0, :, lanes] for t in range(reach)] + [k_ref[:, lanes]], axis=0)
        values = jnp.concatenate([refs[t][1, :, lanes] for t in range(reach)] + [v_ref[:, lanes]], axis=0)
        scores = lax.dot_general(q_ref[:, lanes], keys, (((1,), (1,)), ((), ())),
                                 preferred_element_type=jnp.float32) * scale
        scores = jnp.where(allowed, scores, jnp.float32(-1e30))
        expd = jnp.exp(scores - jnp.max(scores, axis=1, keepdims=True))
        probs = (expd / jnp.sum(expd, axis=1, keepdims=True)).astype(jnp.bfloat16)
        out_ref[:, lanes] = lax.dot_general(probs, values, (((1,), (0,)), ((), ())),
                                            preferred_element_type=jnp.float32).astype(out_ref.dtype)

def window_attention(pos, query, key, value, earlier):
    rows, channels = query.shape
    lanes = 4 * SDIM
    steps = channels // lanes
    flat = pl.BlockSpec((rows, lanes), lambda g, p: (0, g))
    stacked = pl.BlockSpec((2, rows, lanes), lambda g, p: (0, 0, g))
    return pl.pallas_call(
        window_kernel,
        out_shape=jax.ShapeDtypeStruct((rows, channels), jnp.bfloat16),
        grid_spec=pltpu.PrefetchScalarGridSpec(
            num_scalar_prefetch=1, grid=(steps,),
            in_specs=[flat, flat, flat] + [stacked] * len(earlier),
            out_specs=flat),
    )(jnp.reshape(pos, (1,)).astype(jnp.int32), query, key, value, *earlier)


def groups_before(total):
    outer = ("y", "z")
    outer_count = lax.axis_size(outer)
    shape = total.shape
    dealt = total.reshape(outer_count, -1, shape[-1])
    held = lax.all_to_all(dealt, outer, split_axis=0, concat_axis=0, tiled=True)
    prefix = jnp.cumsum(held, axis=0) - held
    back = lax.all_to_all(prefix, outer, split_axis=0, concat_axis=0, tiled=True)
    return back.reshape(shape)


def linear_heads(linear_query, linear_key, linear_value, lin_gain, held):
    rows_dev = linear_query.shape[0]
    group_count = lax.axis_size(GROUP)
    lin_heads = linear_query.shape[1] // FDIM
    own_heads = lin_heads // group_count
    packed = jnp.concatenate(
        [
            linear_query.reshape(rows_dev, group_count, own_heads * FDIM),
            linear_key.reshape(rows_dev, group_count, own_heads * FDIM),
            linear_value.reshape(rows_dev, group_count, own_heads * VDIM),
        ],
        axis=-1,
    )
    got = lax.all_to_all(packed, GROUP, split_axis=1, concat_axis=0, tiled=True)
    rows = got.shape[0]
    got = got.reshape(rows, -1)
    query_bf = got[:, : own_heads * FDIM].reshape(rows, own_heads, FDIM)
    key_bf = got[:, own_heads * FDIM : 2 * own_heads * FDIM].reshape(rows, own_heads, FDIM)
    value_lin = got[:, 2 * own_heads * FDIM :].reshape(rows, own_heads, VDIM).astype(jnp.float32)
    query_lin = query_bf.astype(jnp.float32)
    key_lin = key_bf.astype(jnp.float32)
    total = jnp.einsum(
        "jhf,jhe->hfe", sym_features(key_lin, False), value_lin, precision=lax.Precision.HIGHEST
    )
    before = groups_before(total)
    from_state = jnp.einsum(
        "ihf,hfe->ihe", sym_features(query_lin, True), before, precision=lax.Precision.HIGHEST
    )
    dot_inner = (
        jnp.einsum("ihd,jhd->hij", query_bf, key_bf, preferred_element_type=jnp.float32) * 0.25
    )
    weight = 1.0 + dot_inner + 0.5 * dot_inner * dot_inner
    causal = jnp.arange(rows, dtype=jnp.int32)[:, None] >= jnp.arange(rows, dtype=jnp.int32)[None, :]
    weight = jnp.where(causal[None], weight, jnp.float32(0.0))
    local_sum = jnp.einsum("hij,jhe->ihe", weight, value_lin, precision=lax.Precision.HIGHEST)
    numerator = local_sum + from_state
    inv_rms = lax.rsqrt(jnp.mean(numerator * numerator, axis=-1, keepdims=True) + 1e-05)
    gain_rows = lax.dynamic_slice_in_dim(
        lin_gain.reshape(lin_heads, VDIM), lax.axis_index(GROUP) * own_heads, own_heads, 0
    )
    out = (numerator * inv_rms * gain_rows).astype(jnp.bfloat16)
    out = out.reshape(group_count, rows_dev, own_heads * VDIM)
    back = lax.all_to_all(out, GROUP, split_axis=0, concat_axis=2, tiled=True)
    return back.reshape(rows_dev, lin_heads * VDIM), held


def shards(
    linear_query, linear_key, linear_value, lin_gain, window_query, window_key, window_value
):
    rows_dev = linear_query.shape[0]
    dev_count = lax.axis_size(ALL)
    group_count = lax.axis_size(GROUP)
    device_pos = lax.axis_index(ALL)
    base_row = device_pos * rows_dev
    reach_dev = WINDOW // rows_dev
    channels = window_key.shape[1]
    head_count = channels // SDIM
    lin_heads = linear_query.shape[1] // FDIM

    stacked = jnp.stack([window_key, window_value])
    linear_out, stacked = linear_heads(linear_query, linear_key, linear_value, lin_gain, stacked)
    earlier = [passed_along(stacked, ALL, reach_dev - t) for t in range(reach_dev)]
    window_out = window_attention(device_pos, window_query, window_key, window_value, earlier)
    return (linear_out, window_out)


def solution(mesh):
    seq_count = mesh.shape["seq"]
    sub_count = mesh.shape["sub"]
    lines = seq_count // CORES
    z_count = math.isqrt(lines)
    split_mesh = Mesh(
        np.asarray(mesh.devices).reshape(lines // z_count, z_count, CORES, sub_count), ALL
    )
    rows = P(ALL, None)
    in_specs = (rows, rows, rows, P(), rows, rows, rows)
    out_specs = (rows, rows)
    return jax.shard_map(
        shards, mesh=split_mesh, in_specs=in_specs, out_specs=out_specs, check_vma=False
    )
```

```python
import math

import jax
import jax.numpy as jnp
import numpy as np
from jax import lax
from jax.experimental import pallas as pl
from jax.experimental.pallas import tpu as pltpu
from jax.sharding import Mesh
from jax.sharding import PartitionSpec as P

FDIM = 16
VDIM = 128
SDIM = 128
WINDOW = 512
CORES = 2
FEAT_PAD = 160
ALL = ("y", "z", "core", "sub")
GROUP = ("core", "sub")


def pair_tables(for_query):
    pairs = [(0, 0)] + [(0, a + 1) for a in range(FDIM)]
    pairs += [(a + 1, b + 1) for a in range(FDIM) for b in range(a, FDIM)]
    first = np.zeros((FDIM + 1, FEAT_PAD), np.float32)
    second = np.zeros((FDIM + 1, FEAT_PAD), np.float32)
    for f, (a, b) in enumerate(pairs):
        first[a, f] = 0.5 if (for_query and a == b and a > 0) else 1.0
        second[b, f] = 1.0
    return first, second


def passed_along(shard, axis, by):
    size = lax.axis_size(axis)
    pairs = [(i, i + by) for i in range(size) if 0 <= i + by < size]
    return lax.ppermute(shard, axis, pairs)


def sym_features(vectors, for_query):
    halved = vectors * 0.5
    ext = jnp.concatenate([jnp.ones(halved.shape[:-1] + (1,), jnp.float32), halved], axis=-1)
    first, second = pair_tables(for_query)
    pick = lambda table: jnp.einsum(
        "jhi,if->jhf", ext, jnp.asarray(table), precision=lax.Precision.HIGHEST
    )
    return pick(first) * pick(second)


def window_kernel(pos_ref, q_ref, k_ref, v_ref, *refs):
    reach = len(refs) - 1
    out_ref = refs[-1]
    rows = q_ref.shape[0]
    span = (reach + 1) * rows
    row = lax.broadcasted_iota(jnp.int32, (rows, span), 0)
    rel = lax.broadcasted_iota(jnp.int32, (rows, span), 1) - reach * rows
    first = jnp.zeros((rows, span), jnp.int32) + pos_ref[0] * rows
    allowed = (rel <= row) & (rel > row - WINDOW) & (first + rel >= 0)
    scale = 1.0 / math.sqrt(SDIM)
    for head in range(q_ref.shape[1] // SDIM):
        lanes = pl.ds(head * SDIM, SDIM)
        keys = jnp.concatenate([refs[t][0, :, lanes] for t in range(reach)] + [k_ref[:, lanes]], axis=0)
        values = jnp.concatenate([refs[t][1, :, lanes] for t in range(reach)] + [v_ref[:, lanes]], axis=0)
        scores = lax.dot_general(q_ref[:, lanes], keys, (((1,), (1,)), ((), ())),
                                 preferred_element_type=jnp.float32) * scale
        scores = jnp.where(allowed, scores, jnp.float32(-1e30))
        expd = jnp.exp(scores - jnp.max(scores, axis=1, keepdims=True))
        probs = (expd / jnp.sum(expd, axis=1, keepdims=True)).astype(jnp.bfloat16)
        out_ref[:, lanes] = lax.dot_general(probs, values, (((1,), (0,)), ((), ())),
                                            preferred_element_type=jnp.float32).astype(out_ref.dtype)

def window_attention(pos, query, key, value, arrived, picks):
    rows, channels = query.shape
    lanes = 4 * SDIM
    steps = channels // lanes
    flat = pl.BlockSpec((rows, lanes), lambda g, p: (0, g))
    picked = [
        pl.BlockSpec((None, 2, rows, lanes), lambda g, p, half=half: (half, 0, 0, g))
        for _, half in picks
    ]
    return pl.pallas_call(
        window_kernel,
        out_shape=jax.ShapeDtypeStruct((rows, channels), jnp.bfloat16),
        grid_spec=pltpu.PrefetchScalarGridSpec(
            num_scalar_prefetch=1,
            grid=(steps,),
            in_specs=[flat, flat, flat] + picked,
            out_specs=flat,
        ),
    )(
        jnp.reshape(pos, (1,)).astype(jnp.int32),
        query,
        key,
        value,
        *[arrived[i] for i, _ in picks],
    )


def groups_before(total):
    outer = ("y", "z")
    outer_count = lax.axis_size(outer)
    shape = total.shape
    dealt = total.reshape(outer_count, -1, shape[-1])
    held = lax.all_to_all(dealt, outer, split_axis=0, concat_axis=0, tiled=True)
    prefix = jnp.cumsum(held, axis=0) - held
    back = lax.all_to_all(prefix, outer, split_axis=0, concat_axis=0, tiled=True)
    return back.reshape(shape)


def linear_heads(linear_query, linear_key, linear_value, lin_gain, held):
    rows_dev = linear_query.shape[0]
    group_count = lax.axis_size(GROUP)
    lin_heads = linear_query.shape[1] // FDIM
    own_heads = lin_heads // group_count
    packed = jnp.concatenate(
        [
            linear_query.reshape(rows_dev, group_count, own_heads * FDIM),
            linear_key.reshape(rows_dev, group_count, own_heads * FDIM),
            linear_value.reshape(rows_dev, group_count, own_heads * VDIM),
        ],
        axis=-1,
    )
    got = lax.all_to_all(packed, GROUP, split_axis=1, concat_axis=0, tiled=True)
    rows = got.shape[0]
    got = got.reshape(rows, -1)
    query_bf = got[:, : own_heads * FDIM].reshape(rows, own_heads, FDIM)
    key_bf = got[:, own_heads * FDIM : 2 * own_heads * FDIM].reshape(rows, own_heads, FDIM)
    value_lin = got[:, 2 * own_heads * FDIM :].reshape(rows, own_heads, VDIM).astype(jnp.float32)
    query_lin = query_bf.astype(jnp.float32)
    key_lin = key_bf.astype(jnp.float32)
    total = jnp.einsum(
        "jhf,jhe->hfe", sym_features(key_lin, False), value_lin, precision=lax.Precision.HIGHEST
    )
    before = groups_before(total)
    from_state = jnp.einsum(
        "ihf,hfe->ihe", sym_features(query_lin, True), before, precision=lax.Precision.HIGHEST
    )
    dot_inner = (
        jnp.einsum("ihd,jhd->hij", query_bf, key_bf, preferred_element_type=jnp.float32) * 0.25
    )
    weight = 1.0 + dot_inner + 0.5 * dot_inner * dot_inner
    causal = jnp.arange(rows, dtype=jnp.int32)[:, None] >= jnp.arange(rows, dtype=jnp.int32)[None, :]
    weight = jnp.where(causal[None], weight, jnp.float32(0.0))
    local_sum = jnp.einsum("hij,jhe->ihe", weight, value_lin, precision=lax.Precision.HIGHEST)
    numerator = local_sum + from_state
    inv_rms = lax.rsqrt(jnp.mean(numerator * numerator, axis=-1, keepdims=True) + 1e-05)
    gain_rows = lax.dynamic_slice_in_dim(
        lin_gain.reshape(lin_heads, VDIM), lax.axis_index(GROUP) * own_heads, own_heads, 0
    )
    out = (numerator * inv_rms * gain_rows).astype(jnp.bfloat16)
    out = out.reshape(group_count, rows_dev, own_heads * VDIM)
    back = lax.all_to_all(out, GROUP, split_axis=0, concat_axis=2, tiled=True)
    return back.reshape(rows_dev, lin_heads * VDIM), held


def shards(
    linear_query, linear_key, linear_value, lin_gain, window_query, window_key, window_value
):
    rows_dev = linear_query.shape[0]
    dev_count = lax.axis_size(ALL)
    group_count = lax.axis_size(GROUP)
    device_pos = lax.axis_index(ALL)
    base_row = device_pos * rows_dev
    reach_dev = WINDOW // rows_dev
    channels = window_key.shape[1]
    head_count = channels // SDIM
    lin_heads = linear_query.shape[1] // FDIM

    stacked = jnp.stack([window_key, window_value])
    linear_out, stacked = linear_heads(linear_query, linear_key, linear_value, lin_gain, stacked)
    half = reach_dev // 2
    relayed = passed_along(stacked, ALL, half)
    pair = jnp.stack([stacked, relayed])
    arrived = [passed_along(pair, ALL, k) for k in range(1, half + 1)]
    picks = []
    for t in range(reach_dev):
        distance = reach_dev - t
        picks.append((distance - half - 1, 1) if distance > half else (distance - 1, 0))
    window_out = window_attention(
        device_pos, window_query, window_key, window_value, arrived, picks
    )
    return (linear_out, window_out)


def solution(mesh):
    seq_count = mesh.shape["seq"]
    sub_count = mesh.shape["sub"]
    lines = seq_count // CORES
    z_count = math.isqrt(lines)
    split_mesh = Mesh(
        np.asarray(mesh.devices).reshape(lines // z_count, z_count, CORES, sub_count), ALL
    )
    rows = P(ALL, None)
    in_specs = (rows, rows, rows, P(), rows, rows, rows)
    out_specs = (rows, rows)
    return jax.shard_map(
        shards, mesh=split_mesh, in_specs=in_specs, out_specs=out_specs, check_vma=False
    )
```

```python
import math

import jax
import jax.numpy as jnp
import numpy as np
from jax import lax
from jax.experimental import pallas as pl
from jax.experimental.pallas import tpu as pltpu
from jax.sharding import Mesh
from jax.sharding import PartitionSpec as P

FDIM = 16
VDIM = 128
SDIM = 128
WINDOW = 512
CORES = 2
FEAT_PAD = 160
ALL = ("y", "z", "core", "sub")
GROUP = ("core", "sub")


def pair_tables(for_query):
    pairs = [(0, 0)] + [(0, a + 1) for a in range(FDIM)]
    pairs += [(a + 1, b + 1) for a in range(FDIM) for b in range(a, FDIM)]
    first = np.zeros((FDIM + 1, FEAT_PAD), np.float32)
    second = np.zeros((FDIM + 1, FEAT_PAD), np.float32)
    for f, (a, b) in enumerate(pairs):
        first[a, f] = 0.5 if (for_query and a == b and a > 0) else 1.0
        second[b, f] = 1.0
    return first, second


def passed_along(shard, axis, by):
    size = lax.axis_size(axis)
    pairs = [(i, i + by) for i in range(size) if 0 <= i + by < size]
    return lax.ppermute(shard, axis, pairs)


def sym_features(vectors, for_query):
    halved = vectors * 0.5
    ext = jnp.concatenate([jnp.ones(halved.shape[:-1] + (1,), jnp.float32), halved], axis=-1)
    first, second = pair_tables(for_query)
    pick = lambda table: jnp.einsum(
        "jhi,if->jhf", ext, jnp.asarray(table), precision=lax.Precision.HIGHEST
    )
    return pick(first) * pick(second)


def window_kernel(pos_ref, q_ref, k_ref, v_ref, *refs):
    reach = len(refs) - 1
    out_ref = refs[-1]
    rows = q_ref.shape[0]
    span = (reach + 1) * rows
    row = lax.broadcasted_iota(jnp.int32, (rows, span), 0)
    rel = lax.broadcasted_iota(jnp.int32, (rows, span), 1) - reach * rows
    first = jnp.zeros((rows, span), jnp.int32) + pos_ref[0] * rows
    allowed = (rel <= row) & (rel > row - WINDOW) & (first + rel >= 0)
    scale = 1.0 / math.sqrt(SDIM)
    for head in range(q_ref.shape[1] // SDIM):
        lanes = pl.ds(head * SDIM, SDIM)
        keys = jnp.concatenate([refs[t][0, :, lanes] for t in range(reach)] + [k_ref[:, lanes]], axis=0)
        values = jnp.concatenate([refs[t][1, :, lanes] for t in range(reach)] + [v_ref[:, lanes]], axis=0)
        scores = lax.dot_general(q_ref[:, lanes], keys, (((1,), (1,)), ((), ())),
                                 preferred_element_type=jnp.float32) * scale
        scores = jnp.where(allowed, scores, jnp.float32(-1e30))
        expd = jnp.exp(scores - jnp.max(scores, axis=1, keepdims=True))
        probs = (expd / jnp.sum(expd, axis=1, keepdims=True)).astype(jnp.bfloat16)
        out_ref[:, lanes] = lax.dot_general(probs, values, (((1,), (0,)), ((), ())),
                                            preferred_element_type=jnp.float32).astype(out_ref.dtype)

def window_attention(pos, query, key, value, arrived, picks):
    rows, channels = query.shape
    lanes = 4 * SDIM
    steps = channels // lanes
    flat = pl.BlockSpec((rows, lanes), lambda g, p: (0, g))
    single = pl.BlockSpec((2, rows, lanes), lambda g, p: (0, 0, g))
    picked = [
        single
        if half is None
        else pl.BlockSpec((None, 2, rows, lanes), lambda g, p, half=half: (half, 0, 0, g))
        for _, half in picks
    ]
    return pl.pallas_call(
        window_kernel,
        out_shape=jax.ShapeDtypeStruct((rows, channels), jnp.bfloat16),
        grid_spec=pltpu.PrefetchScalarGridSpec(
            num_scalar_prefetch=1,
            grid=(steps,),
            in_specs=[flat, flat, flat] + picked,
            out_specs=flat,
        ),
    )(
        jnp.reshape(pos, (1,)).astype(jnp.int32),
        query,
        key,
        value,
        *[arrived[i] for i, _ in picks],
    )


def groups_before(total):
    outer = ("y", "z")
    outer_count = lax.axis_size(outer)
    shape = total.shape
    dealt = total.reshape(outer_count, -1, shape[-1])
    held = lax.all_to_all(dealt, outer, split_axis=0, concat_axis=0, tiled=True)
    prefix = jnp.cumsum(held, axis=0) - held
    back = lax.all_to_all(prefix, outer, split_axis=0, concat_axis=0, tiled=True)
    return back.reshape(shape)


def linear_heads(linear_query, linear_key, linear_value, lin_gain, held):
    rows_dev = linear_query.shape[0]
    group_count = lax.axis_size(GROUP)
    lin_heads = linear_query.shape[1] // FDIM
    own_heads = lin_heads // group_count
    packed = jnp.concatenate(
        [
            linear_query.reshape(rows_dev, group_count, own_heads * FDIM),
            linear_key.reshape(rows_dev, group_count, own_heads * FDIM),
            linear_value.reshape(rows_dev, group_count, own_heads * VDIM),
        ],
        axis=-1,
    )
    got = lax.all_to_all(packed, GROUP, split_axis=1, concat_axis=0, tiled=True)
    rows = got.shape[0]
    got = got.reshape(rows, -1)
    query_bf = got[:, : own_heads * FDIM].reshape(rows, own_heads, FDIM)
    key_bf = got[:, own_heads * FDIM : 2 * own_heads * FDIM].reshape(rows, own_heads, FDIM)
    value_lin = got[:, 2 * own_heads * FDIM :].reshape(rows, own_heads, VDIM).astype(jnp.float32)
    query_lin = query_bf.astype(jnp.float32)
    key_lin = key_bf.astype(jnp.float32)
    total = jnp.einsum(
        "jhf,jhe->hfe", sym_features(key_lin, False), value_lin, precision=lax.Precision.HIGHEST
    )
    before = groups_before(total)
    from_state = jnp.einsum(
        "ihf,hfe->ihe", sym_features(query_lin, True), before, precision=lax.Precision.HIGHEST
    )
    dot_inner = (
        jnp.einsum("ihd,jhd->hij", query_bf, key_bf, preferred_element_type=jnp.float32) * 0.25
    )
    weight = 1.0 + dot_inner + 0.5 * dot_inner * dot_inner
    causal = jnp.arange(rows, dtype=jnp.int32)[:, None] >= jnp.arange(rows, dtype=jnp.int32)[None, :]
    weight = jnp.where(causal[None], weight, jnp.float32(0.0))
    local_sum = jnp.einsum("hij,jhe->ihe", weight, value_lin, precision=lax.Precision.HIGHEST)
    numerator = local_sum + from_state
    inv_rms = lax.rsqrt(jnp.mean(numerator * numerator, axis=-1, keepdims=True) + 1e-05)
    gain_rows = lax.dynamic_slice_in_dim(
        lin_gain.reshape(lin_heads, VDIM), lax.axis_index(GROUP) * own_heads, own_heads, 0
    )
    out = (numerator * inv_rms * gain_rows).astype(jnp.bfloat16)
    out = out.reshape(group_count, rows_dev, own_heads * VDIM)
    back = lax.all_to_all(out, GROUP, split_axis=0, concat_axis=2, tiled=True)
    return back.reshape(rows_dev, lin_heads * VDIM), held


def shards(
    linear_query, linear_key, linear_value, lin_gain, window_query, window_key, window_value
):
    rows_dev = linear_query.shape[0]
    dev_count = lax.axis_size(ALL)
    group_count = lax.axis_size(GROUP)
    device_pos = lax.axis_index(ALL)
    base_row = device_pos * rows_dev
    reach_dev = WINDOW // rows_dev
    channels = window_key.shape[1]
    head_count = channels // SDIM
    lin_heads = linear_query.shape[1] // FDIM

    stacked = jnp.stack([window_key, window_value])
    linear_out, stacked = linear_heads(linear_query, linear_key, linear_value, lin_gain, stacked)
    half = reach_dev // 2
    relayed = passed_along(stacked, ALL, half)
    pair = jnp.stack([stacked, relayed])
    arrived = [passed_along(pair, ALL, k) for k in range(1, half)]
    arrived += [relayed, passed_along(relayed, ALL, half)]
    picks = []
    for t in range(reach_dev):
        distance = reach_dev - t
        if distance == reach_dev:
            picks.append((half, None))
        elif distance == half:
            picks.append((half - 1, None))
        elif distance > half:
            picks.append((distance - half - 1, 1))
        else:
            picks.append((distance - 1, 0))
    window_out = window_attention(
        device_pos, window_query, window_key, window_value, arrived, picks
    )
    return (linear_out, window_out)


def solution(mesh):
    seq_count = mesh.shape["seq"]
    sub_count = mesh.shape["sub"]
    lines = seq_count // CORES
    z_count = math.isqrt(lines)
    split_mesh = Mesh(
        np.asarray(mesh.devices).reshape(lines // z_count, z_count, CORES, sub_count), ALL
    )
    rows = P(ALL, None)
    in_specs = (rows, rows, rows, P(), rows, rows, rows)
    out_specs = (rows, rows)
    return jax.shard_map(
        shards, mesh=split_mesh, in_specs=in_specs, out_specs=out_specs, check_vma=False
    )
```

```python
import math

import jax
import jax.numpy as jnp
import numpy as np
from jax import lax
from jax.experimental import pallas as pl
from jax.experimental.pallas import tpu as pltpu
from jax.sharding import Mesh
from jax.sharding import PartitionSpec as P

FDIM = 16
VDIM = 128
SDIM = 128
WINDOW = 512
CORES = 2
FEAT_PAD = 160
ALL = ("y", "z", "core", "sub")
GROUP = ("core", "sub")


def pair_tables(for_query):
    pairs = [(0, 0)] + [(0, a + 1) for a in range(FDIM)]
    pairs += [(a + 1, b + 1) for a in range(FDIM) for b in range(a, FDIM)]
    first = np.zeros((FDIM + 1, FEAT_PAD), np.float32)
    second = np.zeros((FDIM + 1, FEAT_PAD), np.float32)
    for f, (a, b) in enumerate(pairs):
        first[a, f] = 0.5 if (for_query and a == b and a > 0) else 1.0
        second[b, f] = 1.0
    return first, second


def passed_along(shard, axis, by):
    size = lax.axis_size(axis)
    pairs = [(i, i + by) for i in range(size) if 0 <= i + by < size]
    return lax.ppermute(shard, axis, pairs)


def sym_features(vectors, for_query):
    halved = vectors * 0.5
    ext = jnp.concatenate([jnp.ones(halved.shape[:-1] + (1,), jnp.float32), halved], axis=-1)
    first, second = pair_tables(for_query)
    pick = lambda table: jnp.einsum(
        "jhi,if->jhf", ext, jnp.asarray(table), precision=lax.Precision.HIGHEST
    )
    return pick(first) * pick(second)


def window_kernel(pos_ref, q_ref, k_ref, v_ref, *refs):
    reach = len(refs) - 1
    out_ref = refs[-1]
    rows = q_ref.shape[0]
    span = (reach + 1) * rows
    row = lax.broadcasted_iota(jnp.int32, (rows, span), 0)
    rel = lax.broadcasted_iota(jnp.int32, (rows, span), 1) - reach * rows
    first = jnp.zeros((rows, span), jnp.int32) + pos_ref[0] * rows
    allowed = (rel <= row) & (rel > row - WINDOW) & (first + rel >= 0)
    scale = 1.0 / math.sqrt(SDIM)
    for head in range(q_ref.shape[1] // SDIM):
        lanes = pl.ds(head * SDIM, SDIM)
        keys = jnp.concatenate([refs[t][0, :, lanes] for t in range(reach)] + [k_ref[:, lanes]], axis=0)
        values = jnp.concatenate([refs[t][1, :, lanes] for t in range(reach)] + [v_ref[:, lanes]], axis=0)
        scores = lax.dot_general(q_ref[:, lanes], keys, (((1,), (1,)), ((), ())),
                                 preferred_element_type=jnp.float32) * scale
        scores = jnp.where(allowed, scores, jnp.float32(-1e30))
        expd = jnp.exp(scores - jnp.max(scores, axis=1, keepdims=True))
        probs = (expd / jnp.sum(expd, axis=1, keepdims=True)).astype(jnp.bfloat16)
        out_ref[:, lanes] = lax.dot_general(probs, values, (((1,), (0,)), ((), ())),
                                            preferred_element_type=jnp.float32).astype(out_ref.dtype)

def window_attention(pos, query, key, value, arrived, picks):
    rows, channels = query.shape
    lanes = 4 * SDIM
    steps = channels // lanes
    flat = pl.BlockSpec((rows, lanes), lambda g, p: (0, g))
    single = pl.BlockSpec((2, rows, lanes), lambda g, p: (0, 0, g))
    picked = [
        single
        if half is None
        else pl.BlockSpec((None, 2, rows, lanes), lambda g, p, half=half: (half, 0, 0, g))
        for _, half in picks
    ]
    return pl.pallas_call(
        window_kernel,
        out_shape=jax.ShapeDtypeStruct((rows, channels), jnp.bfloat16),
        grid_spec=pltpu.PrefetchScalarGridSpec(
            num_scalar_prefetch=1,
            grid=(steps,),
            in_specs=[flat, flat, flat] + picked,
            out_specs=flat,
        ),
    )(
        jnp.reshape(pos, (1,)).astype(jnp.int32),
        query,
        key,
        value,
        *[arrived[i] for i, _ in picks],
    )


def groups_before(total):
    outer = ("y", "z")
    outer_count = lax.axis_size(outer)
    shape = total.shape
    dealt = total.reshape(outer_count, -1, shape[-1])
    held = lax.all_to_all(dealt, outer, split_axis=0, concat_axis=0, tiled=True)
    prefix = jnp.cumsum(held, axis=0) - held
    back = lax.all_to_all(prefix, outer, split_axis=0, concat_axis=0, tiled=True)
    return back.reshape(shape)


def linear_heads(linear_query, linear_key, linear_value, lin_gain, held):
    rows_dev = linear_query.shape[0]
    group_count = lax.axis_size(GROUP)
    lin_heads = linear_query.shape[1] // FDIM
    own_heads = lin_heads // group_count
    packed = jnp.concatenate(
        [
            linear_query.reshape(rows_dev, group_count, own_heads * FDIM),
            linear_key.reshape(rows_dev, group_count, own_heads * FDIM),
            linear_value.reshape(rows_dev, group_count, own_heads * VDIM),
        ],
        axis=-1,
    )
    packed, held = lax.optimization_barrier((packed, held))
    got = lax.all_to_all(packed, GROUP, split_axis=1, concat_axis=0, tiled=True)
    rows = got.shape[0]
    got = got.reshape(rows, -1)
    query_bf = got[:, : own_heads * FDIM].reshape(rows, own_heads, FDIM)
    key_bf = got[:, own_heads * FDIM : 2 * own_heads * FDIM].reshape(rows, own_heads, FDIM)
    value_lin = got[:, 2 * own_heads * FDIM :].reshape(rows, own_heads, VDIM).astype(jnp.float32)
    query_lin = query_bf.astype(jnp.float32)
    key_lin = key_bf.astype(jnp.float32)
    total = jnp.einsum(
        "jhf,jhe->hfe", sym_features(key_lin, False), value_lin, precision=lax.Precision.HIGHEST
    )
    before = groups_before(total)
    from_state = jnp.einsum(
        "ihf,hfe->ihe", sym_features(query_lin, True), before, precision=lax.Precision.HIGHEST
    )
    dot_inner = (
        jnp.einsum("ihd,jhd->hij", query_bf, key_bf, preferred_element_type=jnp.float32) * 0.25
    )
    weight = 1.0 + dot_inner + 0.5 * dot_inner * dot_inner
    causal = jnp.arange(rows, dtype=jnp.int32)[:, None] >= jnp.arange(rows, dtype=jnp.int32)[None, :]
    weight = jnp.where(causal[None], weight, jnp.float32(0.0))
    local_sum = jnp.einsum("hij,jhe->ihe", weight, value_lin, precision=lax.Precision.HIGHEST)
    numerator = local_sum + from_state
    inv_rms = lax.rsqrt(jnp.mean(numerator * numerator, axis=-1, keepdims=True) + 1e-05)
    gain_rows = lax.dynamic_slice_in_dim(
        lin_gain.reshape(lin_heads, VDIM), lax.axis_index(GROUP) * own_heads, own_heads, 0
    )
    out = (numerator * inv_rms * gain_rows).astype(jnp.bfloat16)
    out = out.reshape(group_count, rows_dev, own_heads * VDIM)
    back = lax.all_to_all(out, GROUP, split_axis=0, concat_axis=2, tiled=True)
    return back.reshape(rows_dev, lin_heads * VDIM), held


def shards(
    linear_query, linear_key, linear_value, lin_gain, window_query, window_key, window_value
):
    rows_dev = linear_query.shape[0]
    dev_count = lax.axis_size(ALL)
    group_count = lax.axis_size(GROUP)
    device_pos = lax.axis_index(ALL)
    base_row = device_pos * rows_dev
    reach_dev = WINDOW // rows_dev
    channels = window_key.shape[1]
    head_count = channels // SDIM
    lin_heads = linear_query.shape[1] // FDIM

    stacked = jnp.stack([window_key, window_value])
    half = reach_dev // 2
    relayed = passed_along(stacked, ALL, half)
    linear_out, relayed = linear_heads(linear_query, linear_key, linear_value, lin_gain, relayed)
    pair = jnp.stack([stacked, relayed])
    arrived = [passed_along(pair, ALL, k) for k in range(1, half)]
    arrived += [relayed, passed_along(relayed, ALL, half)]
    picks = []
    for t in range(reach_dev):
        distance = reach_dev - t
        if distance == reach_dev:
            picks.append((half, None))
        elif distance == half:
            picks.append((half - 1, None))
        elif distance > half:
            picks.append((distance - half - 1, 1))
        else:
            picks.append((distance - 1, 0))
    window_out = window_attention(
        device_pos, window_query, window_key, window_value, arrived, picks
    )
    return (linear_out, window_out)


def solution(mesh):
    seq_count = mesh.shape["seq"]
    sub_count = mesh.shape["sub"]
    lines = seq_count // CORES
    z_count = math.isqrt(lines)
    split_mesh = Mesh(
        np.asarray(mesh.devices).reshape(lines // z_count, z_count, CORES, sub_count), ALL
    )
    rows = P(ALL, None)
    in_specs = (rows, rows, rows, P(), rows, rows, rows)
    out_specs = (rows, rows)
    return jax.shard_map(
        shards, mesh=split_mesh, in_specs=in_specs, out_specs=out_specs, check_vma=False
    )
```

```python
import math

import jax
import jax.numpy as jnp
import numpy as np
from jax import lax
from jax.experimental import pallas as pl
from jax.experimental.pallas import tpu as pltpu
from jax.sharding import Mesh
from jax.sharding import PartitionSpec as P

FDIM = 16
VDIM = 128
SDIM = 128
WINDOW = 512
CORES = 2
FEAT_PAD = 160
ALL = ("y", "z", "pair", "core", "sub")
GROUP = ("pair", "core", "sub")
LINES_PER_GROUP = 2


def pair_tables(for_query):
    pairs = [(0, 0)] + [(0, a + 1) for a in range(FDIM)]
    pairs += [(a + 1, b + 1) for a in range(FDIM) for b in range(a, FDIM)]
    first = np.zeros((FDIM + 1, FEAT_PAD), np.float32)
    second = np.zeros((FDIM + 1, FEAT_PAD), np.float32)
    for f, (a, b) in enumerate(pairs):
        first[a, f] = 0.5 if (for_query and a == b and a > 0) else 1.0
        second[b, f] = 1.0
    return first, second


def passed_along(shard, axis, by):
    size = lax.axis_size(axis)
    pairs = [(i, i + by) for i in range(size) if 0 <= i + by < size]
    return lax.ppermute(shard, axis, pairs)


def sym_features(vectors, for_query):
    halved = vectors * 0.5
    ext = jnp.concatenate([jnp.ones(halved.shape[:-1] + (1,), jnp.float32), halved], axis=-1)
    first, second = pair_tables(for_query)
    pick = lambda table: jnp.einsum(
        "jhi,if->jhf", ext, jnp.asarray(table), precision=lax.Precision.HIGHEST
    )
    return pick(first) * pick(second)


def window_kernel(pos_ref, q_ref, k_ref, v_ref, *refs):
    reach = len(refs) - 1
    out_ref = refs[-1]
    rows = q_ref.shape[0]
    span = (reach + 1) * rows
    row = lax.broadcasted_iota(jnp.int32, (rows, span), 0)
    rel = lax.broadcasted_iota(jnp.int32, (rows, span), 1) - reach * rows
    first = jnp.zeros((rows, span), jnp.int32) + pos_ref[0] * rows
    allowed = (rel <= row) & (rel > row - WINDOW) & (first + rel >= 0)
    scale = 1.0 / math.sqrt(SDIM)
    for head in range(q_ref.shape[1] // SDIM):
        lanes = pl.ds(head * SDIM, SDIM)
        keys = jnp.concatenate([refs[t][0, :, lanes] for t in range(reach)] + [k_ref[:, lanes]], axis=0)
        values = jnp.concatenate([refs[t][1, :, lanes] for t in range(reach)] + [v_ref[:, lanes]], axis=0)
        scores = lax.dot_general(q_ref[:, lanes], keys, (((1,), (1,)), ((), ())),
                                 preferred_element_type=jnp.float32) * scale
        scores = jnp.where(allowed, scores, jnp.float32(-1e30))
        expd = jnp.exp(scores - jnp.max(scores, axis=1, keepdims=True))
        probs = (expd / jnp.sum(expd, axis=1, keepdims=True)).astype(jnp.bfloat16)
        out_ref[:, lanes] = lax.dot_general(probs, values, (((1,), (0,)), ((), ())),
                                            preferred_element_type=jnp.float32).astype(out_ref.dtype)

def window_attention(pos, query, key, value, arrived, picks):
    rows, channels = query.shape
    lanes = 4 * SDIM
    steps = channels // lanes
    flat = pl.BlockSpec((rows, lanes), lambda g, p: (0, g))
    single = pl.BlockSpec((2, rows, lanes), lambda g, p: (0, 0, g))
    picked = [
        single
        if half is None
        else pl.BlockSpec((None, 2, rows, lanes), lambda g, p, half=half: (half, 0, 0, g))
        for _, half in picks
    ]
    return pl.pallas_call(
        window_kernel,
        out_shape=jax.ShapeDtypeStruct((rows, channels), jnp.bfloat16),
        grid_spec=pltpu.PrefetchScalarGridSpec(
            num_scalar_prefetch=1,
            grid=(steps,),
            in_specs=[flat, flat, flat] + picked,
            out_specs=flat,
        ),
    )(
        jnp.reshape(pos, (1,)).astype(jnp.int32),
        query,
        key,
        value,
        *[arrived[i] for i, _ in picks],
    )


def groups_before(total):
    outer = ("y", "z")
    outer_count = lax.axis_size(outer)
    shape = total.shape
    dealt = total.reshape(outer_count, -1, shape[-1])
    held = lax.all_to_all(dealt, outer, split_axis=0, concat_axis=0, tiled=True)
    prefix = jnp.cumsum(held, axis=0) - held
    back = lax.all_to_all(prefix, outer, split_axis=0, concat_axis=0, tiled=True)
    return back.reshape(shape)


def linear_heads(linear_query, linear_key, linear_value, lin_gain, held):
    rows_dev = linear_query.shape[0]
    group_count = lax.axis_size(GROUP)
    lin_heads = linear_query.shape[1] // FDIM
    own_heads = lin_heads // group_count
    packed = jnp.concatenate(
        [
            linear_query.reshape(rows_dev, group_count, own_heads * FDIM),
            linear_key.reshape(rows_dev, group_count, own_heads * FDIM),
            linear_value.reshape(rows_dev, group_count, own_heads * VDIM),
        ],
        axis=-1,
    )
    packed, held = lax.optimization_barrier((packed, held))
    got = lax.all_to_all(packed, GROUP, split_axis=1, concat_axis=0, tiled=True)
    rows = got.shape[0]
    got = got.reshape(rows, -1)
    query_bf = got[:, : own_heads * FDIM].reshape(rows, own_heads, FDIM)
    key_bf = got[:, own_heads * FDIM : 2 * own_heads * FDIM].reshape(rows, own_heads, FDIM)
    value_lin = got[:, 2 * own_heads * FDIM :].reshape(rows, own_heads, VDIM).astype(jnp.float32)
    query_lin = query_bf.astype(jnp.float32)
    key_lin = key_bf.astype(jnp.float32)
    total = jnp.einsum(
        "jhf,jhe->hfe", sym_features(key_lin, False), value_lin, precision=lax.Precision.HIGHEST
    )
    before = groups_before(total)
    from_state = jnp.einsum(
        "ihf,hfe->ihe", sym_features(query_lin, True), before, precision=lax.Precision.HIGHEST
    )
    dot_inner = (
        jnp.einsum("ihd,jhd->hij", query_bf, key_bf, preferred_element_type=jnp.float32) * 0.25
    )
    weight = 1.0 + dot_inner + 0.5 * dot_inner * dot_inner
    causal = jnp.arange(rows, dtype=jnp.int32)[:, None] >= jnp.arange(rows, dtype=jnp.int32)[None, :]
    weight = jnp.where(causal[None], weight, jnp.float32(0.0))
    local_sum = jnp.einsum("hij,jhe->ihe", weight, value_lin, precision=lax.Precision.HIGHEST)
    numerator = local_sum + from_state
    inv_rms = lax.rsqrt(jnp.mean(numerator * numerator, axis=-1, keepdims=True) + 1e-05)
    gain_rows = lax.dynamic_slice_in_dim(
        lin_gain.reshape(lin_heads, VDIM), lax.axis_index(GROUP) * own_heads, own_heads, 0
    )
    out = (numerator * inv_rms * gain_rows).astype(jnp.bfloat16)
    out = out.reshape(group_count, rows_dev, own_heads * VDIM)
    back = lax.all_to_all(out, GROUP, split_axis=0, concat_axis=2, tiled=True)
    return back.reshape(rows_dev, lin_heads * VDIM), held


def shards(
    linear_query, linear_key, linear_value, lin_gain, window_query, window_key, window_value
):
    rows_dev = linear_query.shape[0]
    dev_count = lax.axis_size(ALL)
    group_count = lax.axis_size(GROUP)
    device_pos = lax.axis_index(ALL)
    base_row = device_pos * rows_dev
    reach_dev = WINDOW // rows_dev
    channels = window_key.shape[1]
    head_count = channels // SDIM
    lin_heads = linear_query.shape[1] // FDIM

    stacked = jnp.stack([window_key, window_value])
    half = reach_dev // 2
    relayed = passed_along(stacked, ALL, half)
    linear_out, relayed = linear_heads(linear_query, linear_key, linear_value, lin_gain, relayed)
    pair = jnp.stack([stacked, relayed])
    arrived = [passed_along(pair, ALL, k) for k in range(1, half)]
    arrived += [relayed, passed_along(relayed, ALL, half)]
    picks = []
    for t in range(reach_dev):
        distance = reach_dev - t
        if distance == reach_dev:
            picks.append((half, None))
        elif distance == half:
            picks.append((half - 1, None))
        elif distance > half:
            picks.append((distance - half - 1, 1))
        else:
            picks.append((distance - 1, 0))
    window_out = window_attention(
        device_pos, window_query, window_key, window_value, arrived, picks
    )
    return (linear_out, window_out)


def solution(mesh):
    seq_count = mesh.shape["seq"]
    sub_count = mesh.shape["sub"]
    lines = seq_count // CORES
    z_count = math.isqrt(lines)
    split_mesh = Mesh(
        np.asarray(mesh.devices).reshape(
            lines // z_count,
            z_count // LINES_PER_GROUP,
            LINES_PER_GROUP,
            CORES,
            sub_count,
        ),
        ALL,
    )
    rows = P(ALL, None)
    in_specs = (rows, rows, rows, P(), rows, rows, rows)
    out_specs = (rows, rows)
    return jax.shard_map(
        shards, mesh=split_mesh, in_specs=in_specs, out_specs=out_specs, check_vma=False
    )
```

```python
import math

import jax
import jax.numpy as jnp
import numpy as np
from jax import lax
from jax.experimental import pallas as pl
from jax.experimental.pallas import tpu as pltpu
from jax.sharding import Mesh
from jax.sharding import PartitionSpec as P

FDIM = 16
VDIM = 128
SDIM = 128
WINDOW = 512
CORES = 2
FEAT_PAD = 160
ALL = ("y", "z", "pair", "core", "sub")
GROUP = ("pair", "core", "sub")
LINES_PER_GROUP = 2


def pair_tables(for_query):
    pairs = [(0, 0)] + [(0, a + 1) for a in range(FDIM)]
    pairs += [(a + 1, b + 1) for a in range(FDIM) for b in range(a, FDIM)]
    first = np.zeros((FDIM + 1, FEAT_PAD), np.float32)
    second = np.zeros((FDIM + 1, FEAT_PAD), np.float32)
    for f, (a, b) in enumerate(pairs):
        first[a, f] = 0.5 if (for_query and a == b and a > 0) else 1.0
        second[b, f] = 1.0
    return first, second


def passed_along(shard, axis, by):
    size = lax.axis_size(axis)
    pairs = [(i, i + by) for i in range(size) if 0 <= i + by < size]
    return lax.ppermute(shard, axis, pairs)


def sym_features(vectors, for_query):
    halved = vectors * 0.5
    ext = jnp.concatenate([jnp.ones(halved.shape[:-1] + (1,), jnp.float32), halved], axis=-1)
    first, second = pair_tables(for_query)
    pick = lambda table: jnp.einsum(
        "jhi,if->jhf", ext, jnp.asarray(table), precision=lax.Precision.HIGHEST
    )
    return pick(first) * pick(second)


def window_kernel(pos_ref, q_ref, k_ref, v_ref, *refs):
    reach = len(refs) - 1
    out_ref = refs[-1]
    rows = q_ref.shape[0]
    span = (reach + 1) * rows
    row = lax.broadcasted_iota(jnp.int32, (rows, span), 0)
    rel = lax.broadcasted_iota(jnp.int32, (rows, span), 1) - reach * rows
    first = jnp.zeros((rows, span), jnp.int32) + pos_ref[0] * rows
    allowed = (rel <= row) & (rel > row - WINDOW) & (first + rel >= 0)
    scale = 1.0 / math.sqrt(SDIM)
    for head in range(q_ref.shape[1] // SDIM):
        lanes = pl.ds(head * SDIM, SDIM)
        keys = jnp.concatenate([refs[t][0, :, lanes] for t in range(reach)] + [k_ref[:, lanes]], axis=0)
        values = jnp.concatenate([refs[t][1, :, lanes] for t in range(reach)] + [v_ref[:, lanes]], axis=0)
        scores = lax.dot_general(q_ref[:, lanes], keys, (((1,), (1,)), ((), ())),
                                 preferred_element_type=jnp.float32) * scale
        scores = jnp.where(allowed, scores, jnp.float32(-1e30))
        expd = jnp.exp(scores - jnp.max(scores, axis=1, keepdims=True))
        probs = (expd / jnp.sum(expd, axis=1, keepdims=True)).astype(jnp.bfloat16)
        out_ref[:, lanes] = lax.dot_general(probs, values, (((1,), (0,)), ((), ())),
                                            preferred_element_type=jnp.float32).astype(out_ref.dtype)

def window_attention(pos, query, key, value, arrived, picks):
    rows, channels = query.shape
    lanes = 4 * SDIM
    steps = channels // lanes
    flat = pl.BlockSpec((rows, lanes), lambda g, p: (0, g))
    single = pl.BlockSpec((2, rows, lanes), lambda g, p: (0, 0, g))
    picked = [
        single
        if half is None
        else pl.BlockSpec((None, 2, rows, lanes), lambda g, p, half=half: (half, 0, 0, g))
        for _, half in picks
    ]
    return pl.pallas_call(
        window_kernel,
        out_shape=jax.ShapeDtypeStruct((rows, channels), jnp.bfloat16),
        grid_spec=pltpu.PrefetchScalarGridSpec(
            num_scalar_prefetch=1,
            grid=(steps,),
            in_specs=[flat, flat, flat] + picked,
            out_specs=flat,
        ),
    )(
        jnp.reshape(pos, (1,)).astype(jnp.int32),
        query,
        key,
        value,
        *[arrived[i] for i, _ in picks],
    )


def groups_before(total):
    outer = ("y", "z")
    outer_count = lax.axis_size(outer)
    shape = total.shape
    dealt = total.reshape(outer_count, -1, shape[-1])
    held = lax.all_to_all(dealt, outer, split_axis=0, concat_axis=0, tiled=True)
    prefix = jnp.cumsum(held, axis=0) - held
    back = lax.all_to_all(prefix, outer, split_axis=0, concat_axis=0, tiled=True)
    return back.reshape(shape)


def linear_heads(linear_query, linear_key, linear_value, lin_gain, held, finish):
    rows_dev = linear_query.shape[0]
    group_count = lax.axis_size(GROUP)
    lin_heads = linear_query.shape[1] // FDIM
    own_heads = lin_heads // group_count
    packed = jnp.concatenate(
        [
            linear_query.reshape(rows_dev, group_count, own_heads * FDIM),
            linear_key.reshape(rows_dev, group_count, own_heads * FDIM),
            linear_value.reshape(rows_dev, group_count, own_heads * VDIM),
        ],
        axis=-1,
    )
    packed, held = lax.optimization_barrier((packed, held))
    got = lax.all_to_all(packed, GROUP, split_axis=1, concat_axis=0, tiled=True)
    rows = got.shape[0]
    got = got.reshape(rows, -1)
    query_bf = got[:, : own_heads * FDIM].reshape(rows, own_heads, FDIM)
    key_bf = got[:, own_heads * FDIM : 2 * own_heads * FDIM].reshape(rows, own_heads, FDIM)
    value_lin = got[:, 2 * own_heads * FDIM :].reshape(rows, own_heads, VDIM).astype(jnp.float32)
    query_lin = query_bf.astype(jnp.float32)
    key_lin = key_bf.astype(jnp.float32)
    total = jnp.einsum(
        "jhf,jhe->hfe", sym_features(key_lin, False), value_lin, precision=lax.Precision.HIGHEST
    )
    before = groups_before(total)
    before, finished = lax.optimization_barrier((before, finish(held)))
    from_state = jnp.einsum(
        "ihf,hfe->ihe", sym_features(query_lin, True), before, precision=lax.Precision.HIGHEST
    )
    dot_inner = (
        jnp.einsum("ihd,jhd->hij", query_bf, key_bf, preferred_element_type=jnp.float32) * 0.25
    )
    weight = 1.0 + dot_inner + 0.5 * dot_inner * dot_inner
    causal = jnp.arange(rows, dtype=jnp.int32)[:, None] >= jnp.arange(rows, dtype=jnp.int32)[None, :]
    weight = jnp.where(causal[None], weight, jnp.float32(0.0))
    local_sum = jnp.einsum("hij,jhe->ihe", weight, value_lin, precision=lax.Precision.HIGHEST)
    numerator = local_sum + from_state
    inv_rms = lax.rsqrt(jnp.mean(numerator * numerator, axis=-1, keepdims=True) + 1e-05)
    gain_rows = lax.dynamic_slice_in_dim(
        lin_gain.reshape(lin_heads, VDIM), lax.axis_index(GROUP) * own_heads, own_heads, 0
    )
    out = (numerator * inv_rms * gain_rows).astype(jnp.bfloat16)
    out = out.reshape(group_count, rows_dev, own_heads * VDIM)
    back = lax.all_to_all(out, GROUP, split_axis=0, concat_axis=2, tiled=True)
    return back.reshape(rows_dev, lin_heads * VDIM), finished


def shards(
    linear_query, linear_key, linear_value, lin_gain, window_query, window_key, window_value
):
    rows_dev = linear_query.shape[0]
    dev_count = lax.axis_size(ALL)
    group_count = lax.axis_size(GROUP)
    device_pos = lax.axis_index(ALL)
    base_row = device_pos * rows_dev
    reach_dev = WINDOW // rows_dev
    channels = window_key.shape[1]
    head_count = channels // SDIM
    lin_heads = linear_query.shape[1] // FDIM

    stacked = jnp.stack([window_key, window_value])
    half = reach_dev // 2
    relayed = passed_along(stacked, ALL, half)

    def finish(relayed):
        pair = jnp.stack([stacked, relayed])
        arrived = [passed_along(pair, ALL, k) for k in range(1, half)]
        arrived += [relayed, passed_along(relayed, ALL, half)]
        picks = []
        for t in range(reach_dev):
            distance = reach_dev - t
            if distance == reach_dev:
                picks.append((half, None))
            elif distance == half:
                picks.append((half - 1, None))
            elif distance > half:
                picks.append((distance - half - 1, 1))
            else:
                picks.append((distance - 1, 0))
        return window_attention(
            device_pos, window_query, window_key, window_value, arrived, picks
        )

    linear_out, window_out = linear_heads(
        linear_query, linear_key, linear_value, lin_gain, relayed, finish
    )
    return (linear_out, window_out)


def solution(mesh):
    seq_count = mesh.shape["seq"]
    sub_count = mesh.shape["sub"]
    lines = seq_count // CORES
    z_count = math.isqrt(lines)
    split_mesh = Mesh(
        np.asarray(mesh.devices).reshape(
            lines // z_count,
            z_count // LINES_PER_GROUP,
            LINES_PER_GROUP,
            CORES,
            sub_count,
        ),
        ALL,
    )
    rows = P(ALL, None)
    in_specs = (rows, rows, rows, P(), rows, rows, rows)
    out_specs = (rows, rows)
    return jax.shard_map(
        shards, mesh=split_mesh, in_specs=in_specs, out_specs=out_specs, check_vma=False
    )
```

```python
import math

import jax
import jax.numpy as jnp
import numpy as np
from jax import lax
from jax.experimental import pallas as pl
from jax.experimental.pallas import tpu as pltpu
from jax.sharding import Mesh
from jax.sharding import PartitionSpec as P

FDIM = 16
VDIM = 128
SDIM = 128
WINDOW = 512
CORES = 2
FEAT_PAD = 160
ALL = ("y", "z", "pair", "core", "sub")
GROUP = ("pair", "core", "sub")
LINES_PER_GROUP = 2


def pair_tables(for_query):
    pairs = [(0, 0)] + [(0, a + 1) for a in range(FDIM)]
    pairs += [(a + 1, b + 1) for a in range(FDIM) for b in range(a, FDIM)]
    first = np.zeros((FDIM + 1, FEAT_PAD), np.float32)
    second = np.zeros((FDIM + 1, FEAT_PAD), np.float32)
    for f, (a, b) in enumerate(pairs):
        first[a, f] = 0.5 if (for_query and a == b and a > 0) else 1.0
        second[b, f] = 1.0
    return first, second


def passed_along(shard, axis, by):
    size = lax.axis_size(axis)
    pairs = [(i, i + by) for i in range(size) if 0 <= i + by < size]
    return lax.ppermute(shard, axis, pairs)


def sym_features(vectors, for_query):
    halved = vectors * 0.5
    ext = jnp.concatenate([jnp.ones(halved.shape[:-1] + (1,), jnp.float32), halved], axis=-1)
    first, second = pair_tables(for_query)
    pick = lambda table: jnp.einsum(
        "jhi,if->jhf", ext, jnp.asarray(table), precision=lax.Precision.HIGHEST
    )
    return pick(first) * pick(second)


def window_kernel(pos_ref, q_ref, k_ref, v_ref, *refs):
    reach = len(refs) - 1
    out_ref = refs[-1]
    rows = q_ref.shape[0]
    span = (reach + 1) * rows
    row = lax.broadcasted_iota(jnp.int32, (rows, span), 0)
    rel = lax.broadcasted_iota(jnp.int32, (rows, span), 1) - reach * rows
    first = jnp.zeros((rows, span), jnp.int32) + pos_ref[0] * rows
    allowed = (rel <= row) & (rel > row - WINDOW) & (first + rel >= 0)
    scale = 1.0 / math.sqrt(SDIM)
    for head in range(q_ref.shape[1] // SDIM):
        lanes = pl.ds(head * SDIM, SDIM)
        keys = jnp.concatenate([refs[t][0, :, lanes] for t in range(reach)] + [k_ref[:, lanes]], axis=0)
        values = jnp.concatenate([refs[t][1, :, lanes] for t in range(reach)] + [v_ref[:, lanes]], axis=0)
        scores = lax.dot_general(q_ref[:, lanes], keys, (((1,), (1,)), ((), ())),
                                 preferred_element_type=jnp.float32) * scale
        scores = jnp.where(allowed, scores, jnp.float32(-1e30))
        expd = jnp.exp(scores - jnp.max(scores, axis=1, keepdims=True))
        probs = (expd / jnp.sum(expd, axis=1, keepdims=True)).astype(jnp.bfloat16)
        out_ref[:, lanes] = lax.dot_general(probs, values, (((1,), (0,)), ((), ())),
                                            preferred_element_type=jnp.float32).astype(out_ref.dtype)

def window_attention(pos, query, key, value, arrived, picks):
    rows, channels = query.shape
    lanes = 4 * SDIM
    steps = channels // lanes
    flat = pl.BlockSpec((rows, lanes), lambda g, p: (0, g))
    single = pl.BlockSpec((2, rows, lanes), lambda g, p: (0, 0, g))
    picked = [
        single
        if half is None
        else pl.BlockSpec((None, 2, rows, lanes), lambda g, p, half=half: (half, 0, 0, g))
        for _, half in picks
    ]
    return pl.pallas_call(
        window_kernel,
        out_shape=jax.ShapeDtypeStruct((rows, channels), jnp.bfloat16),
        grid_spec=pltpu.PrefetchScalarGridSpec(
            num_scalar_prefetch=1,
            grid=(steps,),
            in_specs=[flat, flat, flat] + picked,
            out_specs=flat,
        ),
    )(
        jnp.reshape(pos, (1,)).astype(jnp.int32),
        query,
        key,
        value,
        *[arrived[i] for i, _ in picks],
    )


def groups_before(total):
    outer = ("y", "z")
    outer_count = lax.axis_size(outer)
    shape = total.shape
    dealt = total.reshape(outer_count, -1, shape[-1])
    held = lax.all_to_all(dealt, outer, split_axis=0, concat_axis=0, tiled=True)
    prefix = jnp.cumsum(held, axis=0) - held
    back = lax.all_to_all(prefix, outer, split_axis=0, concat_axis=0, tiled=True)
    return back.reshape(shape)


def linear_heads(linear_query, linear_key, linear_value, lin_gain, held):
    rows_dev = linear_query.shape[0]
    group_count = lax.axis_size(GROUP)
    lin_heads = linear_query.shape[1] // FDIM
    own_heads = lin_heads // group_count
    packed = jnp.concatenate(
        [
            linear_query.reshape(rows_dev, group_count, own_heads * FDIM),
            linear_key.reshape(rows_dev, group_count, own_heads * FDIM),
            linear_value.reshape(rows_dev, group_count, own_heads * VDIM),
        ],
        axis=-1,
    )
    packed, held = lax.optimization_barrier((packed, held))
    got = lax.all_to_all(packed, GROUP, split_axis=1, concat_axis=0, tiled=True)
    rows = got.shape[0]
    got = got.reshape(rows, -1)
    query_bf = got[:, : own_heads * FDIM].reshape(rows, own_heads, FDIM)
    key_bf = got[:, own_heads * FDIM : 2 * own_heads * FDIM].reshape(rows, own_heads, FDIM)
    value_lin = got[:, 2 * own_heads * FDIM :].reshape(rows, own_heads, VDIM).astype(jnp.float32)
    query_lin = query_bf.astype(jnp.float32)
    key_lin = key_bf.astype(jnp.float32)
    total = jnp.einsum(
        "jhf,jhe->hfe", sym_features(key_lin, False), value_lin, precision=lax.Precision.HIGHEST
    )
    total, held = lax.optimization_barrier((total, held))
    before = groups_before(total)
    from_state = jnp.einsum(
        "ihf,hfe->ihe", sym_features(query_lin, True), before, precision=lax.Precision.HIGHEST
    )
    dot_inner = (
        jnp.einsum("ihd,jhd->hij", query_bf, key_bf, preferred_element_type=jnp.float32) * 0.25
    )
    weight = 1.0 + dot_inner + 0.5 * dot_inner * dot_inner
    causal = jnp.arange(rows, dtype=jnp.int32)[:, None] >= jnp.arange(rows, dtype=jnp.int32)[None, :]
    weight = jnp.where(causal[None], weight, jnp.float32(0.0))
    local_sum = jnp.einsum("hij,jhe->ihe", weight, value_lin, precision=lax.Precision.HIGHEST)
    numerator = local_sum + from_state
    inv_rms = lax.rsqrt(jnp.mean(numerator * numerator, axis=-1, keepdims=True) + 1e-05)
    gain_rows = lax.dynamic_slice_in_dim(
        lin_gain.reshape(lin_heads, VDIM), lax.axis_index(GROUP) * own_heads, own_heads, 0
    )
    out = (numerator * inv_rms * gain_rows).astype(jnp.bfloat16)
    out = out.reshape(group_count, rows_dev, own_heads * VDIM)
    back = lax.all_to_all(out, GROUP, split_axis=0, concat_axis=2, tiled=True)
    return back.reshape(rows_dev, lin_heads * VDIM), held


def shards(
    linear_query, linear_key, linear_value, lin_gain, window_query, window_key, window_value
):
    rows_dev = linear_query.shape[0]
    dev_count = lax.axis_size(ALL)
    group_count = lax.axis_size(GROUP)
    device_pos = lax.axis_index(ALL)
    base_row = device_pos * rows_dev
    reach_dev = WINDOW // rows_dev
    channels = window_key.shape[1]
    head_count = channels // SDIM
    lin_heads = linear_query.shape[1] // FDIM

    stacked = jnp.stack([window_key, window_value])
    half = reach_dev // 2
    relayed = passed_along(stacked, ALL, half)
    linear_out, relayed = linear_heads(linear_query, linear_key, linear_value, lin_gain, relayed)
    pair = jnp.stack([stacked, relayed])
    arrived = [passed_along(pair, ALL, k) for k in range(1, half)]
    arrived += [relayed, passed_along(relayed, ALL, half)]
    picks = []
    for t in range(reach_dev):
        distance = reach_dev - t
        if distance == reach_dev:
            picks.append((half, None))
        elif distance == half:
            picks.append((half - 1, None))
        elif distance > half:
            picks.append((distance - half - 1, 1))
        else:
            picks.append((distance - 1, 0))
    window_out = window_attention(
        device_pos, window_query, window_key, window_value, arrived, picks
    )
    return (linear_out, window_out)


def solution(mesh):
    seq_count = mesh.shape["seq"]
    sub_count = mesh.shape["sub"]
    lines = seq_count // CORES
    z_count = math.isqrt(lines)
    split_mesh = Mesh(
        np.asarray(mesh.devices).reshape(
            lines // z_count,
            z_count // LINES_PER_GROUP,
            LINES_PER_GROUP,
            CORES,
            sub_count,
        ),
        ALL,
    )
    rows = P(ALL, None)
    in_specs = (rows, rows, rows, P(), rows, rows, rows)
    out_specs = (rows, rows)
    return jax.shard_map(
        shards, mesh=split_mesh, in_specs=in_specs, out_specs=out_specs, check_vma=False
    )
```

```python
import math

import jax
import jax.numpy as jnp
import numpy as np
from jax import lax
from jax.experimental import pallas as pl
from jax.experimental.pallas import tpu as pltpu
from jax.sharding import Mesh
from jax.sharding import PartitionSpec as P

FDIM = 16
VDIM = 128
SDIM = 128
WINDOW = 512
CORES = 2
FEAT_PAD = 160
ALL = ("y", "z", "pair", "core", "sub")
GROUP = ("pair", "core", "sub")
LINES_PER_GROUP = 2


def pair_tables(for_query):
    pairs = [(0, 0)] + [(0, a + 1) for a in range(FDIM)]
    pairs += [(a + 1, b + 1) for a in range(FDIM) for b in range(a, FDIM)]
    first = np.zeros((FDIM + 1, FEAT_PAD), np.float32)
    second = np.zeros((FDIM + 1, FEAT_PAD), np.float32)
    for f, (a, b) in enumerate(pairs):
        first[a, f] = 0.5 if (for_query and a == b and a > 0) else 1.0
        second[b, f] = 1.0
    return first, second


def passed_along(shard, axis, by):
    size = lax.axis_size(axis)
    pairs = [(i, i + by) for i in range(size) if 0 <= i + by < size]
    return lax.ppermute(shard, axis, pairs)


def sym_features(vectors, for_query):
    halved = vectors * 0.5
    ext = jnp.concatenate([jnp.ones(halved.shape[:-1] + (1,), jnp.float32), halved], axis=-1)
    first, second = pair_tables(for_query)
    pick = lambda table: jnp.einsum(
        "jhi,if->jhf", ext, jnp.asarray(table), precision=lax.Precision.HIGHEST
    )
    return pick(first) * pick(second)


def window_kernel(pos_ref, q_ref, k_ref, v_ref, *refs):
    reach = len(refs) - 1
    out_ref = refs[-1]
    rows = q_ref.shape[0]
    span = (reach + 1) * rows
    row = lax.broadcasted_iota(jnp.int32, (rows, span), 0)
    rel = lax.broadcasted_iota(jnp.int32, (rows, span), 1) - reach * rows
    first = jnp.zeros((rows, span), jnp.int32) + pos_ref[0] * rows
    allowed = (rel <= row) & (rel > row - WINDOW) & (first + rel >= 0)
    scale = 1.0 / math.sqrt(SDIM)
    for head in range(q_ref.shape[1] // SDIM):
        lanes = pl.ds(head * SDIM, SDIM)
        keys = jnp.concatenate([refs[t][0, :, lanes] for t in range(reach)] + [k_ref[:, lanes]], axis=0)
        values = jnp.concatenate([refs[t][1, :, lanes] for t in range(reach)] + [v_ref[:, lanes]], axis=0)
        scores = lax.dot_general(q_ref[:, lanes], keys, (((1,), (1,)), ((), ())),
                                 preferred_element_type=jnp.float32) * scale
        scores = jnp.where(allowed, scores, jnp.float32(-1e30))
        expd = jnp.exp(scores - jnp.max(scores, axis=1, keepdims=True))
        probs = (expd / jnp.sum(expd, axis=1, keepdims=True)).astype(jnp.bfloat16)
        out_ref[:, lanes] = lax.dot_general(probs, values, (((1,), (0,)), ((), ())),
                                            preferred_element_type=jnp.float32).astype(out_ref.dtype)

def window_attention(pos, query, key, value, arrived, picks):
    rows, channels = query.shape
    lanes = 4 * SDIM
    steps = channels // lanes
    flat = pl.BlockSpec((rows, lanes), lambda g, p: (0, g))
    single = pl.BlockSpec((2, rows, lanes), lambda g, p: (0, 0, g))
    picked = [
        single
        if half is None
        else pl.BlockSpec((None, 2, rows, lanes), lambda g, p, half=half: (half, 0, 0, g))
        for _, half in picks
    ]
    return pl.pallas_call(
        window_kernel,
        out_shape=jax.ShapeDtypeStruct((rows, channels), jnp.bfloat16),
        grid_spec=pltpu.PrefetchScalarGridSpec(
            num_scalar_prefetch=1,
            grid=(steps,),
            in_specs=[flat, flat, flat] + picked,
            out_specs=flat,
        ),
    )(
        jnp.reshape(pos, (1,)).astype(jnp.int32),
        query,
        key,
        value,
        *[arrived[i] for i, _ in picks],
    )


def groups_before(total, tag):
    outer = ("y", "z")
    outer_count = lax.axis_size(outer)
    shape = total.shape
    dealt = total.reshape(outer_count, -1, shape[-1])
    held = lax.all_to_all(dealt, outer, split_axis=0, concat_axis=0, tiled=True)
    held, tag = lax.optimization_barrier((held, tag))
    prefix = jnp.cumsum(held, axis=0) - held
    back = lax.all_to_all(prefix, outer, split_axis=0, concat_axis=0, tiled=True)
    return back.reshape(shape), tag


def linear_heads(linear_query, linear_key, linear_value, lin_gain, held):
    rows_dev = linear_query.shape[0]
    group_count = lax.axis_size(GROUP)
    lin_heads = linear_query.shape[1] // FDIM
    own_heads = lin_heads // group_count
    packed = jnp.concatenate(
        [
            linear_query.reshape(rows_dev, group_count, own_heads * FDIM),
            linear_key.reshape(rows_dev, group_count, own_heads * FDIM),
            linear_value.reshape(rows_dev, group_count, own_heads * VDIM),
        ],
        axis=-1,
    )
    packed, held = lax.optimization_barrier((packed, held))
    got = lax.all_to_all(packed, GROUP, split_axis=1, concat_axis=0, tiled=True)
    rows = got.shape[0]
    got = got.reshape(rows, -1)
    query_bf = got[:, : own_heads * FDIM].reshape(rows, own_heads, FDIM)
    key_bf = got[:, own_heads * FDIM : 2 * own_heads * FDIM].reshape(rows, own_heads, FDIM)
    value_lin = got[:, 2 * own_heads * FDIM :].reshape(rows, own_heads, VDIM).astype(jnp.float32)
    query_lin = query_bf.astype(jnp.float32)
    key_lin = key_bf.astype(jnp.float32)
    total = jnp.einsum(
        "jhf,jhe->hfe", sym_features(key_lin, False), value_lin, precision=lax.Precision.HIGHEST
    )
    before, (query_bf, key_bf, value_lin) = groups_before(total, (query_bf, key_bf, value_lin))
    from_state = jnp.einsum(
        "ihf,hfe->ihe", sym_features(query_lin, True), before, precision=lax.Precision.HIGHEST
    )
    dot_inner = (
        jnp.einsum("ihd,jhd->hij", query_bf, key_bf, preferred_element_type=jnp.float32) * 0.25
    )
    weight = 1.0 + dot_inner + 0.5 * dot_inner * dot_inner
    causal = jnp.arange(rows, dtype=jnp.int32)[:, None] >= jnp.arange(rows, dtype=jnp.int32)[None, :]
    weight = jnp.where(causal[None], weight, jnp.float32(0.0))
    local_sum = jnp.einsum("hij,jhe->ihe", weight, value_lin, precision=lax.Precision.HIGHEST)
    numerator = local_sum + from_state
    inv_rms = lax.rsqrt(jnp.mean(numerator * numerator, axis=-1, keepdims=True) + 1e-05)
    gain_rows = lax.dynamic_slice_in_dim(
        lin_gain.reshape(lin_heads, VDIM), lax.axis_index(GROUP) * own_heads, own_heads, 0
    )
    out = (numerator * inv_rms * gain_rows).astype(jnp.bfloat16)
    out = out.reshape(group_count, rows_dev, own_heads * VDIM)
    back = lax.all_to_all(out, GROUP, split_axis=0, concat_axis=2, tiled=True)
    return back.reshape(rows_dev, lin_heads * VDIM), held


def shards(
    linear_query, linear_key, linear_value, lin_gain, window_query, window_key, window_value
):
    rows_dev = linear_query.shape[0]
    dev_count = lax.axis_size(ALL)
    group_count = lax.axis_size(GROUP)
    device_pos = lax.axis_index(ALL)
    base_row = device_pos * rows_dev
    reach_dev = WINDOW // rows_dev
    channels = window_key.shape[1]
    head_count = channels // SDIM
    lin_heads = linear_query.shape[1] // FDIM

    stacked = jnp.stack([window_key, window_value])
    half = reach_dev // 2
    relayed = passed_along(stacked, ALL, half)
    linear_out, relayed = linear_heads(linear_query, linear_key, linear_value, lin_gain, relayed)
    pair = jnp.stack([stacked, relayed])
    arrived = [passed_along(pair, ALL, k) for k in range(1, half)]
    arrived += [relayed, passed_along(relayed, ALL, half)]
    picks = []
    for t in range(reach_dev):
        distance = reach_dev - t
        if distance == reach_dev:
            picks.append((half, None))
        elif distance == half:
            picks.append((half - 1, None))
        elif distance > half:
            picks.append((distance - half - 1, 1))
        else:
            picks.append((distance - 1, 0))
    window_out = window_attention(
        device_pos, window_query, window_key, window_value, arrived, picks
    )
    return (linear_out, window_out)


def solution(mesh):
    seq_count = mesh.shape["seq"]
    sub_count = mesh.shape["sub"]
    lines = seq_count // CORES
    z_count = math.isqrt(lines)
    split_mesh = Mesh(
        np.asarray(mesh.devices).reshape(
            lines // z_count,
            z_count // LINES_PER_GROUP,
            LINES_PER_GROUP,
            CORES,
            sub_count,
        ),
        ALL,
    )
    rows = P(ALL, None)
    in_specs = (rows, rows, rows, P(), rows, rows, rows)
    out_specs = (rows, rows)
    return jax.shard_map(
        shards, mesh=split_mesh, in_specs=in_specs, out_specs=out_specs, check_vma=False
    )
```

```python
import math

import jax
import jax.numpy as jnp
import numpy as np
from jax import lax
from jax.experimental import pallas as pl
from jax.experimental.pallas import tpu as pltpu
from jax.sharding import Mesh
from jax.sharding import PartitionSpec as P

FDIM = 16
VDIM = 128
SDIM = 128
WINDOW = 512
CORES = 2
FEAT_PAD = 160
ALL = ("y", "z", "pair", "core", "sub")
GROUP = ("pair", "core", "sub")
LINES_PER_GROUP = 2


def pair_tables(for_query):
    pairs = [(0, 0)] + [(0, a + 1) for a in range(FDIM)]
    pairs += [(a + 1, b + 1) for a in range(FDIM) for b in range(a, FDIM)]
    first = np.zeros((FDIM + 1, FEAT_PAD), np.float32)
    second = np.zeros((FDIM + 1, FEAT_PAD), np.float32)
    for f, (a, b) in enumerate(pairs):
        first[a, f] = 0.5 if (for_query and a == b and a > 0) else 1.0
        second[b, f] = 1.0
    return first, second


def passed_along(shard, axis, by):
    size = lax.axis_size(axis)
    pairs = [(i, i + by) for i in range(size) if 0 <= i + by < size]
    return lax.ppermute(shard, axis, pairs)


def sym_features(vectors, for_query):
    halved = vectors * 0.5
    ext = jnp.concatenate([jnp.ones(halved.shape[:-1] + (1,), jnp.float32), halved], axis=-1)
    first, second = pair_tables(for_query)
    pick = lambda table: jnp.einsum(
        "jhi,if->jhf", ext, jnp.asarray(table), precision=lax.Precision.HIGHEST
    )
    return pick(first) * pick(second)


def window_kernel(pos_ref, q_ref, k_ref, v_ref, *refs):
    reach = len(refs) - 1
    out_ref = refs[-1]
    rows = q_ref.shape[0]
    span = (reach + 1) * rows
    row = lax.broadcasted_iota(jnp.int32, (rows, span), 0)
    rel = lax.broadcasted_iota(jnp.int32, (rows, span), 1) - reach * rows
    first = jnp.zeros((rows, span), jnp.int32) + pos_ref[0] * rows
    allowed = (rel <= row) & (rel > row - WINDOW) & (first + rel >= 0)
    scale = 1.0 / math.sqrt(SDIM)
    for head in range(q_ref.shape[1] // SDIM):
        lanes = pl.ds(head * SDIM, SDIM)
        keys = jnp.concatenate([refs[t][0, :, lanes] for t in range(reach)] + [k_ref[:, lanes]], axis=0)
        values = jnp.concatenate([refs[t][1, :, lanes] for t in range(reach)] + [v_ref[:, lanes]], axis=0)
        scores = lax.dot_general(q_ref[:, lanes], keys, (((1,), (1,)), ((), ())),
                                 preferred_element_type=jnp.float32) * scale
        scores = jnp.where(allowed, scores, jnp.float32(-1e30))
        expd = jnp.exp(scores - jnp.max(scores, axis=1, keepdims=True))
        probs = (expd / jnp.sum(expd, axis=1, keepdims=True)).astype(jnp.bfloat16)
        out_ref[:, lanes] = lax.dot_general(probs, values, (((1,), (0,)), ((), ())),
                                            preferred_element_type=jnp.float32).astype(out_ref.dtype)

def window_attention(pos, query, key, value, arrived, picks):
    rows, channels = query.shape
    lanes = 2 * SDIM
    steps = channels // lanes
    flat = pl.BlockSpec((rows, lanes), lambda g, p: (0, g))
    single = pl.BlockSpec((2, rows, lanes), lambda g, p: (0, 0, g))
    picked = [
        single
        if half is None
        else pl.BlockSpec((None, 2, rows, lanes), lambda g, p, half=half: (half, 0, 0, g))
        for _, half in picks
    ]
    return pl.pallas_call(
        window_kernel,
        out_shape=jax.ShapeDtypeStruct((rows, channels), jnp.bfloat16),
        grid_spec=pltpu.PrefetchScalarGridSpec(
            num_scalar_prefetch=1,
            grid=(steps,),
            in_specs=[flat, flat, flat] + picked,
            out_specs=flat,
        ),
    )(
        jnp.reshape(pos, (1,)).astype(jnp.int32),
        query,
        key,
        value,
        *[arrived[i] for i, _ in picks],
    )


def groups_before(total):
    outer = ("y", "z")
    outer_count = lax.axis_size(outer)
    shape = total.shape
    dealt = total.reshape(outer_count, -1, shape[-1])
    held = lax.all_to_all(dealt, outer, split_axis=0, concat_axis=0, tiled=True)
    prefix = jnp.cumsum(held, axis=0) - held
    back = lax.all_to_all(prefix, outer, split_axis=0, concat_axis=0, tiled=True)
    return back.reshape(shape)


def linear_heads(linear_query, linear_key, linear_value, lin_gain, held):
    rows_dev = linear_query.shape[0]
    group_count = lax.axis_size(GROUP)
    lin_heads = linear_query.shape[1] // FDIM
    own_heads = lin_heads // group_count
    packed = jnp.concatenate(
        [
            linear_query.reshape(rows_dev, group_count, own_heads * FDIM),
            linear_key.reshape(rows_dev, group_count, own_heads * FDIM),
            linear_value.reshape(rows_dev, group_count, own_heads * VDIM),
        ],
        axis=-1,
    )
    packed, held = lax.optimization_barrier((packed, held))
    got = lax.all_to_all(packed, GROUP, split_axis=1, concat_axis=0, tiled=True)
    rows = got.shape[0]
    got = got.reshape(rows, -1)
    query_bf = got[:, : own_heads * FDIM].reshape(rows, own_heads, FDIM)
    key_bf = got[:, own_heads * FDIM : 2 * own_heads * FDIM].reshape(rows, own_heads, FDIM)
    value_lin = got[:, 2 * own_heads * FDIM :].reshape(rows, own_heads, VDIM).astype(jnp.float32)
    query_lin = query_bf.astype(jnp.float32)
    key_lin = key_bf.astype(jnp.float32)
    total = jnp.einsum(
        "jhf,jhe->hfe", sym_features(key_lin, False), value_lin, precision=lax.Precision.HIGHEST
    )
    before = groups_before(total)
    from_state = jnp.einsum(
        "ihf,hfe->ihe", sym_features(query_lin, True), before, precision=lax.Precision.HIGHEST
    )
    dot_inner = (
        jnp.einsum("ihd,jhd->hij", query_bf, key_bf, preferred_element_type=jnp.float32) * 0.25
    )
    weight = 1.0 + dot_inner + 0.5 * dot_inner * dot_inner
    causal = jnp.arange(rows, dtype=jnp.int32)[:, None] >= jnp.arange(rows, dtype=jnp.int32)[None, :]
    weight = jnp.where(causal[None], weight, jnp.float32(0.0))
    local_sum = jnp.einsum("hij,jhe->ihe", weight, value_lin, precision=lax.Precision.HIGHEST)
    numerator = local_sum + from_state
    inv_rms = lax.rsqrt(jnp.mean(numerator * numerator, axis=-1, keepdims=True) + 1e-05)
    gain_rows = lax.dynamic_slice_in_dim(
        lin_gain.reshape(lin_heads, VDIM), lax.axis_index(GROUP) * own_heads, own_heads, 0
    )
    out = (numerator * inv_rms * gain_rows).astype(jnp.bfloat16)
    out = out.reshape(group_count, rows_dev, own_heads * VDIM)
    back = lax.all_to_all(out, GROUP, split_axis=0, concat_axis=2, tiled=True)
    return back.reshape(rows_dev, lin_heads * VDIM), held


def shards(
    linear_query, linear_key, linear_value, lin_gain, window_query, window_key, window_value
):
    rows_dev = linear_query.shape[0]
    dev_count = lax.axis_size(ALL)
    group_count = lax.axis_size(GROUP)
    device_pos = lax.axis_index(ALL)
    base_row = device_pos * rows_dev
    reach_dev = WINDOW // rows_dev
    channels = window_key.shape[1]
    head_count = channels // SDIM
    lin_heads = linear_query.shape[1] // FDIM

    stacked = jnp.stack([window_key, window_value])
    half = reach_dev // 2
    relayed = passed_along(stacked, ALL, half)
    linear_out, relayed = linear_heads(linear_query, linear_key, linear_value, lin_gain, relayed)
    pair = jnp.stack([stacked, relayed])
    arrived = [passed_along(pair, ALL, k) for k in range(1, half)]
    arrived += [relayed, passed_along(relayed, ALL, half)]
    picks = []
    for t in range(reach_dev):
        distance = reach_dev - t
        if distance == reach_dev:
            picks.append((half, None))
        elif distance == half:
            picks.append((half - 1, None))
        elif distance > half:
            picks.append((distance - half - 1, 1))
        else:
            picks.append((distance - 1, 0))
    window_out = window_attention(
        device_pos, window_query, window_key, window_value, arrived, picks
    )
    return (linear_out, window_out)


def solution(mesh):
    seq_count = mesh.shape["seq"]
    sub_count = mesh.shape["sub"]
    lines = seq_count // CORES
    z_count = math.isqrt(lines)
    split_mesh = Mesh(
        np.asarray(mesh.devices).reshape(
            lines // z_count,
            z_count // LINES_PER_GROUP,
            LINES_PER_GROUP,
            CORES,
            sub_count,
        ),
        ALL,
    )
    rows = P(ALL, None)
    in_specs = (rows, rows, rows, P(), rows, rows, rows)
    out_specs = (rows, rows)
    return jax.shard_map(
        shards, mesh=split_mesh, in_specs=in_specs, out_specs=out_specs, check_vma=False
    )
```

```python
import math

import jax
import jax.numpy as jnp
import numpy as np
from jax import lax
from jax.experimental import pallas as pl
from jax.experimental.pallas import tpu as pltpu
from jax.sharding import Mesh
from jax.sharding import PartitionSpec as P

FDIM = 16
VDIM = 128
SDIM = 128
WINDOW = 512
CORES = 2
FEAT_PAD = 160
ALL = ("y", "z", "pair", "core", "sub")
GROUP = ("pair", "core", "sub")
LINES_PER_GROUP = 2


def pair_tables(for_query):
    pairs = [(0, 0)] + [(0, a + 1) for a in range(FDIM)]
    pairs += [(a + 1, b + 1) for a in range(FDIM) for b in range(a, FDIM)]
    first = np.zeros((FDIM + 1, FEAT_PAD), np.float32)
    second = np.zeros((FDIM + 1, FEAT_PAD), np.float32)
    for f, (a, b) in enumerate(pairs):
        first[a, f] = 0.5 if (for_query and a == b and a > 0) else 1.0
        second[b, f] = 1.0
    return first, second


def passed_along(shard, axis, by):
    size = lax.axis_size(axis)
    pairs = [(i, i + by) for i in range(size) if 0 <= i + by < size]
    return lax.ppermute(shard, axis, pairs)


def sym_features(vectors, for_query):
    halved = vectors * 0.5
    ext = jnp.concatenate([jnp.ones(halved.shape[:-1] + (1,), jnp.float32), halved], axis=-1)
    first, second = pair_tables(for_query)
    pick = lambda table: jnp.einsum(
        "jhi,if->jhf", ext, jnp.asarray(table), precision=lax.Precision.HIGHEST
    )
    return pick(first) * pick(second)


def window_kernel(pos_ref, q_ref, k_ref, v_ref, *refs):
    reach = len(refs) - 1
    out_ref = refs[-1]
    rows = q_ref.shape[0]
    span = (reach + 1) * rows
    row = lax.broadcasted_iota(jnp.int32, (rows, span), 0)
    rel = lax.broadcasted_iota(jnp.int32, (rows, span), 1) - reach * rows
    first = jnp.zeros((rows, span), jnp.int32) + pos_ref[0] * rows
    allowed = (rel <= row) & (rel > row - WINDOW) & (first + rel >= 0)
    scale = 1.0 / math.sqrt(SDIM)
    for head in range(q_ref.shape[1] // SDIM):
        lanes = pl.ds(head * SDIM, SDIM)
        keys = jnp.concatenate([refs[t][0, :, lanes] for t in range(reach)] + [k_ref[:, lanes]], axis=0)
        values = jnp.concatenate([refs[t][1, :, lanes] for t in range(reach)] + [v_ref[:, lanes]], axis=0)
        scores = lax.dot_general(q_ref[:, lanes], keys, (((1,), (1,)), ((), ())),
                                 preferred_element_type=jnp.float32) * scale
        scores = jnp.where(allowed, scores, jnp.float32(-1e30))
        expd = jnp.exp(scores - jnp.max(scores, axis=1, keepdims=True))
        probs = (expd / jnp.sum(expd, axis=1, keepdims=True)).astype(jnp.bfloat16)
        out_ref[:, lanes] = lax.dot_general(probs, values, (((1,), (0,)), ((), ())),
                                            preferred_element_type=jnp.float32).astype(out_ref.dtype)

def window_attention(pos, query, key, value, arrived, picks):
    rows, channels = query.shape
    lanes = 8 * SDIM
    steps = channels // lanes
    flat = pl.BlockSpec((rows, lanes), lambda g, p: (0, g))
    single = pl.BlockSpec((2, rows, lanes), lambda g, p: (0, 0, g))
    picked = [
        single
        if half is None
        else pl.BlockSpec((None, 2, rows, lanes), lambda g, p, half=half: (half, 0, 0, g))
        for _, half in picks
    ]
    return pl.pallas_call(
        window_kernel,
        out_shape=jax.ShapeDtypeStruct((rows, channels), jnp.bfloat16),
        grid_spec=pltpu.PrefetchScalarGridSpec(
            num_scalar_prefetch=1,
            grid=(steps,),
            in_specs=[flat, flat, flat] + picked,
            out_specs=flat,
        ),
    )(
        jnp.reshape(pos, (1,)).astype(jnp.int32),
        query,
        key,
        value,
        *[arrived[i] for i, _ in picks],
    )


def groups_before(total):
    outer = ("y", "z")
    outer_count = lax.axis_size(outer)
    shape = total.shape
    dealt = total.reshape(outer_count, -1, shape[-1])
    held = lax.all_to_all(dealt, outer, split_axis=0, concat_axis=0, tiled=True)
    prefix = jnp.cumsum(held, axis=0) - held
    back = lax.all_to_all(prefix, outer, split_axis=0, concat_axis=0, tiled=True)
    return back.reshape(shape)


def linear_heads(linear_query, linear_key, linear_value, lin_gain, held):
    rows_dev = linear_query.shape[0]
    group_count = lax.axis_size(GROUP)
    lin_heads = linear_query.shape[1] // FDIM
    own_heads = lin_heads // group_count
    packed = jnp.concatenate(
        [
            linear_query.reshape(rows_dev, group_count, own_heads * FDIM),
            linear_key.reshape(rows_dev, group_count, own_heads * FDIM),
            linear_value.reshape(rows_dev, group_count, own_heads * VDIM),
        ],
        axis=-1,
    )
    packed, held = lax.optimization_barrier((packed, held))
    got = lax.all_to_all(packed, GROUP, split_axis=1, concat_axis=0, tiled=True)
    rows = got.shape[0]
    got = got.reshape(rows, -1)
    query_bf = got[:, : own_heads * FDIM].reshape(rows, own_heads, FDIM)
    key_bf = got[:, own_heads * FDIM : 2 * own_heads * FDIM].reshape(rows, own_heads, FDIM)
    value_lin = got[:, 2 * own_heads * FDIM :].reshape(rows, own_heads, VDIM).astype(jnp.float32)
    query_lin = query_bf.astype(jnp.float32)
    key_lin = key_bf.astype(jnp.float32)
    total = jnp.einsum(
        "jhf,jhe->hfe", sym_features(key_lin, False), value_lin, precision=lax.Precision.HIGHEST
    )
    before = groups_before(total)
    from_state = jnp.einsum(
        "ihf,hfe->ihe", sym_features(query_lin, True), before, precision=lax.Precision.HIGHEST
    )
    dot_inner = (
        jnp.einsum("ihd,jhd->hij", query_bf, key_bf, preferred_element_type=jnp.float32) * 0.25
    )
    weight = 1.0 + dot_inner + 0.5 * dot_inner * dot_inner
    causal = jnp.arange(rows, dtype=jnp.int32)[:, None] >= jnp.arange(rows, dtype=jnp.int32)[None, :]
    weight = jnp.where(causal[None], weight, jnp.float32(0.0))
    local_sum = jnp.einsum("hij,jhe->ihe", weight, value_lin, precision=lax.Precision.HIGHEST)
    numerator = local_sum + from_state
    inv_rms = lax.rsqrt(jnp.mean(numerator * numerator, axis=-1, keepdims=True) + 1e-05)
    gain_rows = lax.dynamic_slice_in_dim(
        lin_gain.reshape(lin_heads, VDIM), lax.axis_index(GROUP) * own_heads, own_heads, 0
    )
    out = (numerator * inv_rms * gain_rows).astype(jnp.bfloat16)
    out = out.reshape(group_count, rows_dev, own_heads * VDIM)
    back = lax.all_to_all(out, GROUP, split_axis=0, concat_axis=2, tiled=True)
    return back.reshape(rows_dev, lin_heads * VDIM), held


def shards(
    linear_query, linear_key, linear_value, lin_gain, window_query, window_key, window_value
):
    rows_dev = linear_query.shape[0]
    dev_count = lax.axis_size(ALL)
    group_count = lax.axis_size(GROUP)
    device_pos = lax.axis_index(ALL)
    base_row = device_pos * rows_dev
    reach_dev = WINDOW // rows_dev
    channels = window_key.shape[1]
    head_count = channels // SDIM
    lin_heads = linear_query.shape[1] // FDIM

    stacked = jnp.stack([window_key, window_value])
    half = reach_dev // 2
    relayed = passed_along(stacked, ALL, half)
    linear_out, relayed = linear_heads(linear_query, linear_key, linear_value, lin_gain, relayed)
    pair = jnp.stack([stacked, relayed])
    arrived = [passed_along(pair, ALL, k) for k in range(1, half)]
    arrived += [relayed, passed_along(relayed, ALL, half)]
    picks = []
    for t in range(reach_dev):
        distance = reach_dev - t
        if distance == reach_dev:
            picks.append((half, None))
        elif distance == half:
            picks.append((half - 1, None))
        elif distance > half:
            picks.append((distance - half - 1, 1))
        else:
            picks.append((distance - 1, 0))
    window_out = window_attention(
        device_pos, window_query, window_key, window_value, arrived, picks
    )
    return (linear_out, window_out)


def solution(mesh):
    seq_count = mesh.shape["seq"]
    sub_count = mesh.shape["sub"]
    lines = seq_count // CORES
    z_count = math.isqrt(lines)
    split_mesh = Mesh(
        np.asarray(mesh.devices).reshape(
            lines // z_count,
            z_count // LINES_PER_GROUP,
            LINES_PER_GROUP,
            CORES,
            sub_count,
        ),
        ALL,
    )
    rows = P(ALL, None)
    in_specs = (rows, rows, rows, P(), rows, rows, rows)
    out_specs = (rows, rows)
    return jax.shard_map(
        shards, mesh=split_mesh, in_specs=in_specs, out_specs=out_specs, check_vma=False
    )
```
